256 devices in a mesh: dp: 16 (over z_lo, y), tensor: 16 (over x, z_hi, core).
Axes of the slice: x: 4, y: 4, z: 8 (z_hi: 2, z_lo: 4; z = z_hi * 4 + z_lo), core: 2. Of those that a mesh axis runs over, the one named last changes fastest.
Arguments:
- hidden: bfloat16 [12288, 2048], P(('dp', 'tensor')), may hold values from -6 to 6
- lengths: int32 [64], replicated, may hold values from 1 to 384, as said below
- prefix_id: int32 [64], replicated, may hold values from 0 to 1
- placement_perm: int32 [64], replicated, may hold values from 0 to 63, as said below
- prefix_owner: int32 [2], replicated, may hold values from 0 to 15, as said below
- prefix_cache: bfloat16 [16, 2, 4096, 2048], P('dp', None, None, 'tensor'), may hold values from -400 to 400
- qkv_weight: bfloat16 [3, 2048, 2048], P(None, None, 'tensor')
- q_gain: float32 [2048], replicated, may hold values from 0.1 to 1.9
- k_gain: float32 [2048], replicated, may hold values from 0.1 to 1.9
- out_weight: bfloat16 [2048, 2048], P('tensor'), may hold values from -0.125 to 0.125
- attn_gain: float32 [2048], replicated, may hold values from 0.1 to 1.9
- gate_up_weight: bfloat16 [2, 2048, 8192], P(None, None, 'tensor'), may hold values from -0.125 to 0.125
- down_weight: bfloat16 [8192, 2048], P('tensor'), may hold values from -0.0625 to 0.0625
- mlp_gain: float32 [2048], replicated, may hold values from 0.1 to 1.9
Outputs:
- hidden_out: bfloat16 [12288, 2048], P(('dp', 'tensor'))
- suffix_kv: bfloat16 [2, 12288, 2048], P(None, 'dp', 'tensor')
The draws below stay inside these ranges and needn't reach their ends.
Inputs may be any that keep to these rules, and one draw needn't show every extreme that they name: `lengths`: the requests that placement_perm puts into one group hold at most 768 tokens together; in every draw some group holds exactly 768. `placement_perm`: A permutation of the 64 requests. `prefix_owner`: two different dp indices, one of which is always the last dp index.
All inputs are finite; a program needn't handle non-finite values.
Results may differ from the reference program's by a relative error of at most 0.025.
Values may be sent and summed in bfloat16 or wider, within the bound.
No kernel may reach another device: no remote copies, remote signals or barrier semaphores. Data moves between devices by JAX's collectives and lax.ppermute only.
A program may use at most 128 MiB of HBM per device.

```python
import jax
import jax.numpy as jnp
from jax import lax

D = 2048
HEADS = 16
HD = 128
FF = 8192
CAP = 768
REQ_GRP = 4
PLEN = 4096
REQS = 64
N_DP = 16


def request_plan(key):
    plan_key = jax.random.fold_in(key, 11)
    key_perm, key_busy, key_slot, key_head, key_floor = jax.random.split(plan_key, 5)
    groups_total = REQS // REQ_GRP
    request_order = jax.random.permutation(key_perm, REQS).astype(jnp.int32)
    busiest = jax.random.randint(key_busy, (), 0, groups_total)
    quarter = CAP // 4
    slot_len = jax.random.randint(key_slot, (groups_total, REQ_GRP), 1, quarter + 1)
    first_len = jax.random.randint(key_head, (), 1, quarter)
    busy_row = jnp.stack([first_len, quarter - first_len, jnp.int32(quarter), jnp.int32(CAP // 2)]).astype(jnp.int32)
    group_ids = jnp.arange(groups_total, dtype=jnp.int32)
    slot_len = jnp.where(group_ids[:, None] == busiest, busy_row[None, :], slot_len)
    floor_group = (busiest + 1 + jax.random.randint(key_floor, (), 0, groups_total - 1)) % groups_total
    first_slot = (group_ids[:, None] == floor_group) & (jnp.arange(REQ_GRP, dtype=jnp.int32)[None, :] == 0)
    slot_len = jnp.where(first_slot, 1, slot_len).astype(jnp.int32)
    lengths = jnp.zeros((REQS,), jnp.int32).at[request_order].set(slot_len.reshape(-1))
    return (request_order, lengths)


def draw_lengths(key, part):
    return request_plan(key)[1]


def draw_placement_perm(key, part):
    return request_plan(key)[0]


def draw_prefix_owner(key, part):
    owner_key = jax.random.fold_in(key, 23)
    key_other, key_order = jax.random.split(owner_key, 2)
    groups_total = REQS // REQ_GRP
    last_owner = jnp.int32(groups_total - 1)
    other_owner = jax.random.randint(key_other, (), 0, groups_total - 1).astype(jnp.int32)
    flipped = jax.random.randint(key_order, (), 0, 2) == 1
    first_owner = jnp.where(flipped, last_owner, other_owner)
    second_owner = jnp.where(flipped, other_owner, last_owner)
    return jnp.stack([first_owner, second_owner]).astype(jnp.int32)


def draw_prefix_cache(key, part):
    cache_key = jax.random.fold_in(key, 31)
    key_base = jax.random.fold_in(cache_key, 0)
    groups_total = REQS // REQ_GRP
    base = jnp.clip(jax.random.normal(key_base, (groups_total, 2, PLEN, D), jnp.float32), -4.0, 4.0)
    return base.astype(jnp.bfloat16)


def draw_qkv_weight(key, part):
    weight_key = jax.random.fold_in(key, 41)
    key_base, key_spread = jax.random.split(weight_key, 2)
    column = jnp.arange(D, dtype=jnp.float32) / (D - 1)
    spread = jax.random.uniform(key_spread, (3, 1, D), jnp.float32, 0.0, 1.0)
    base = jnp.clip(jax.random.normal(key_base, (3, D, D), jnp.float32), -5.0, 5.0)
    rising = jnp.power(3.0, 0.5 * column)
    values = base * D ** (-0.5) * jnp.power(10.0, spread) * rising[None, None, :]
    return values.astype(jnp.bfloat16)


def plant(values, own_key, smallest, largest):
    longest = values.shape.index(max(values.shape))
    spots = []
    for shift in (0, 1):
        where = [jax.random.randint(jax.random.fold_in(own_key, axis), (), 0, length) for axis, length in enumerate(values.shape)]
        where[longest] = (where[longest] + shift) % values.shape[longest]
        spots.append(tuple(where))
    return values.at[spots[0]].set(smallest).at[spots[1]].set(largest)


def shard_levels(stream_key, dims, cuts, low, largest):
    factor_of = 1.0
    for dim, blocks in cuts:
        steps = jax.random.uniform(jax.random.fold_in(jax.random.fold_in(stream_key, 6), dim), (blocks,), jnp.float32, low / len(cuts), largest / len(cuts))
        factor_of = factor_of * jnp.repeat(jnp.exp(steps), dims[dim] // blocks).reshape((-1,) + (1,) * (len(dims) - 1 - dim))
    return factor_of


def noise(key, shape, scale, bound, shards=(), kind=jnp.bfloat16):
    values = jax.random.normal(key, shape, jnp.float32) * scale
    if len(shards) > 0:
        values = shard_levels(key, shape, shards, -0.22, 0.18) * values
    return jnp.clip(values, min=-bound, max=bound).astype(kind)


def setup_inputs(seed: int = 0) -> dict:
    key_of = jax.random.split(jax.random.key(seed), 15)
    return {
        "hidden": noise(key_of[0], (REQS // REQ_GRP * CAP, D), 1.0, 6.0, ((0, 256),)),
        "lengths": draw_lengths(jax.random.fold_in(key_of[14], 71), 0),
        "prefix_id": plant(jax.random.randint(key_of[2], (REQS,), 0, 2), jax.random.fold_in(key_of[2], 1), 0, 1).astype(jnp.int32),
        "placement_perm": draw_placement_perm(jax.random.fold_in(key_of[14], 71), 0),
        "prefix_owner": draw_prefix_owner(jax.random.fold_in(key_of[14], 71), 0),
        "prefix_cache": draw_prefix_cache(jax.random.fold_in(key_of[14], 71), 0),
        "qkv_weight": draw_qkv_weight(jax.random.fold_in(key_of[14], 71), 0),
        "q_gain": jnp.clip(1.0 + 0.18 * jax.random.normal(key_of[7], (D,), jnp.float32), 0.1, 1.9),
        "k_gain": jnp.clip(1.0 + 0.18 * jax.random.normal(key_of[8], (D,), jnp.float32), 0.1, 1.9),
        "out_weight": noise(key_of[9], (D, D), D ** -0.5, 0.125, ((0, 16),)),
        "attn_gain": jnp.clip(1.0 + 0.18 * jax.random.normal(key_of[10], (D,), jnp.float32), 0.1, 1.9),
        "gate_up_weight": noise(key_of[11], (2, D, FF), D ** -0.5, 0.125, ((2, 16),)),
        "down_weight": noise(key_of[12], (FF, D), FF ** -0.5, 0.0625, ((0, 16),)),
        "mlp_gain": jnp.clip(1.0 + 0.18 * jax.random.normal(key_of[13], (D,), jnp.float32), 0.1, 1.9),
    }


ROPE_BASE = 500000.0
EPSILON = 1e-06
MASKED_SCORE = -1e+30

def slot_plan(lengths, prefix_id, placement_perm, group_index):
    requests = lax.dynamic_slice(placement_perm, (group_index * REQ_GRP,), (REQ_GRP,))
    req_sizes = jnp.take(lengths, requests)
    starts = jnp.cumsum(req_sizes) - req_sizes
    slot_ids = jnp.arange(CAP, dtype=jnp.int32)
    inside = ((slot_ids[None, :] >= starts[:, None]) & (slot_ids[None, :] < (starts + req_sizes)[:, None])).astype(jnp.int32)
    live_slots = lax.optimization_barrier(jnp.sum(inside, axis=0)) > 0
    numbers = jnp.arange(1, REQ_GRP + 1, dtype=jnp.int32)
    owner_req = lax.optimization_barrier(jnp.sum(inside * numbers[:, None], axis=0)) - 1
    offsets = slot_ids - lax.optimization_barrier(jnp.sum(inside * starts[:, None], axis=0))
    prefix_pick = lax.optimization_barrier(jnp.sum(inside * jnp.take(prefix_id, requests)[:, None], axis=0))
    return (slot_ids, live_slots, owner_req, offsets, prefix_pick)

def rotate(values, offsets):
    half_dim = HD // 2
    inverse = jnp.power(ROPE_BASE, -2.0 * jnp.arange(half_dim, dtype=jnp.float32) / HD)
    angles = (offsets.astype(jnp.float32) + PLEN)[:, None] * inverse[None, :]
    cosine = jnp.cos(angles)[:, None, :]
    sine_part = jnp.sin(angles)[:, None, :]
    front_half = values[..., :half_dim]
    back_half = values[..., half_dim:]
    return jnp.concatenate([front_half * cosine - back_half * sine_part, back_half * cosine + front_half * sine_part], axis=-1)

def rms_scale(values, gain):
    mean_square = lax.optimization_barrier(jnp.mean(values * values, axis=-1, keepdims=True))
    return values * lax.rsqrt(mean_square + EPSILON) * gain

def rounded(values):
    return lax.optimization_barrier(values.astype(jnp.bfloat16)).astype(jnp.float32)

def reference(hidden, lengths, prefix_id, placement_perm, prefix_owner, prefix_cache, qkv_weight, q_gain, k_gain, out_weight, attn_gain, gate_up_weight, down_weight, mlp_gain):
    score_scale = HD ** (-0.5)
    chosen = jnp.take(prefix_cache, prefix_owner, axis=0).astype(jnp.float32).reshape(2, 2, PLEN, HEADS, HD)

    def one_group(group_index):
        slot_ids, live_slots, owner_req, offsets, prefix_pick = slot_plan(lengths, prefix_id, placement_perm, group_index)
        group_rows = lax.dynamic_slice_in_dim(hidden, group_index * CAP, CAP, 0)
        queries = jnp.dot(group_rows, qkv_weight[0], preferred_element_type=jnp.float32)
        key_rows = jnp.dot(group_rows, qkv_weight[1], preferred_element_type=jnp.float32)
        value_rows = jnp.dot(group_rows, qkv_weight[2], preferred_element_type=jnp.float32)
        queries = rotate(rms_scale(queries, q_gain).reshape(CAP, HEADS, HD), offsets)
        key_bf = rotate(rms_scale(key_rows, k_gain).reshape(CAP, HEADS, HD), offsets).astype(jnp.bfloat16)
        value_bf = value_rows.astype(jnp.bfloat16).reshape(CAP, HEADS, HD)
        query_f = rounded(queries)
        key_f = key_bf.astype(jnp.float32)
        value_f = value_bf.astype(jnp.float32)
        score_zero = jnp.einsum('chd,khd->hck', query_f, chosen[0, 0]) * score_scale
        score_one = jnp.einsum('chd,khd->hck', query_f, chosen[1, 0]) * score_scale
        pick_zero = (prefix_pick == 0)[None, :, None]
        pre_scores = jnp.where(pick_zero, score_zero, score_one)
        suf_scores = jnp.einsum('chd,khd->hck', query_f, key_f) * score_scale
        visible = (owner_req[:, None] == owner_req[None, :]) & live_slots[None, :] & (slot_ids[None, :] <= slot_ids[:, None])
        suf_scores = jnp.where(visible[None], suf_scores, MASKED_SCORE)
        running_max = jnp.maximum(lax.optimization_barrier(jnp.max(pre_scores, axis=-1, keepdims=True)), lax.optimization_barrier(jnp.max(suf_scores, axis=-1, keepdims=True)))
        pre_weights = jnp.exp(pre_scores - running_max)
        suf_weights = jnp.exp(suf_scores - running_max)
        weight_sum = lax.optimization_barrier(jnp.sum(pre_weights, axis=-1, keepdims=True)) + lax.optimization_barrier(jnp.sum(suf_weights, axis=-1, keepdims=True))
        pre_round = rounded(pre_weights)
        pre_out = jnp.where(pick_zero, jnp.einsum('hck,khd->hcd', pre_round, chosen[0, 1]), jnp.einsum('hck,khd->hcd', pre_round, chosen[1, 1]))
        suf_out = jnp.einsum('hck,khd->hcd', rounded(suf_weights), value_f)
        attended = ((pre_out + suf_out) / weight_sum).astype(jnp.bfloat16)
        attended = attended.transpose(1, 0, 2).reshape(CAP, D)
        attn = jnp.dot(attended, out_weight, preferred_element_type=jnp.float32)
        mid = (group_rows.astype(jnp.float32) + rms_scale(attn, attn_gain)).astype(jnp.bfloat16)
        gate = jnp.dot(mid, gate_up_weight[0], preferred_element_type=jnp.float32)
        upward = jnp.dot(mid, gate_up_weight[1], preferred_element_type=jnp.float32)
        activated = (jax.nn.silu(gate) * upward).astype(jnp.bfloat16)
        mlp_term = jnp.dot(activated, down_weight, preferred_element_type=jnp.float32)
        result = mid.astype(jnp.float32) + rms_scale(mlp_term, mlp_gain)
        hidden_out = jnp.where(live_slots[:, None], result, 0.0).astype(jnp.bfloat16)
        key_out = jnp.where(live_slots[:, None], key_bf.reshape(CAP, D), 0.0).astype(jnp.bfloat16)
        value_out = jnp.where(live_slots[:, None], value_bf.reshape(CAP, D), 0.0).astype(jnp.bfloat16)
        return (hidden_out, key_out, value_out)
    outs_all = lax.map(one_group, jnp.arange(N_DP, dtype=jnp.int32))
    hidden_out = outs_all[0].reshape(N_DP * CAP, D)
    suffix_kv = jnp.stack([outs_all[1].reshape(N_DP * CAP, D), outs_all[2].reshape(N_DP * CAP, D)])
    return (hidden_out, suffix_kv)
```

```python
import jax
import jax.numpy as jnp
from jax import lax
from jax.sharding import PartitionSpec as P

D = 2048
HD = 128
CAP = 768
REQ_GRP = 4
PLEN = 4096


ROPE_BASE = 500000.0
EPSILON = 1e-06
MASKED_SCORE = -1e30


def from_root(shard, axis, root):
    mine = lax.axis_index(axis) == root
    return lax.psum(jnp.where(mine, shard, jnp.zeros_like(shard)), axis)


def _pairs(fn, n=16):
    return [(t, fn(t) % n) for t in range(n)]


def tensor_coords():
    t = lax.axis_index("tensor")
    return t // 4, (t // 2) % 2, t % 2


def ag_tensor(block):
    x_i, zh, c = tensor_coords()
    other = lax.ppermute(block, "tensor", _pairs(lambda t: t ^ 2))
    pair = jnp.where(zh == 0, jnp.stack([block, other]), jnp.stack([other, block]))
    from_x = [lax.ppermute(pair, "tensor", _pairs(lambda t, k=k: t + 4 * k)) for k in (3, 2, 1)]
    quad = jnp.roll(jnp.stack([pair] + from_x), x_i, axis=0)
    mate = lax.ppermute(quad, "tensor", _pairs(lambda t: t ^ 1))
    full = jnp.where(c == 0, jnp.stack([quad, mate], axis=2), jnp.stack([mate, quad], axis=2))
    return full.reshape((-1,) + block.shape[1:])


def rs_tensor(rows):
    x_i, zh, c = tensor_coords()
    grid = rows.reshape((4, 2, 2, -1) + rows.shape[1:])
    mine = jnp.take(grid, c, axis=2).astype(jnp.float32)
    theirs = jnp.take(grid, 1 - c, axis=2).astype(jnp.bfloat16)
    summed = mine + lax.ppermute(theirs, "tensor", _pairs(lambda t: t ^ 1)).astype(jnp.float32)
    rel = jnp.roll(summed, -x_i, axis=0)
    total = rel[0]
    for k in (1, 2, 3):
        sent = rel[k].astype(jnp.bfloat16)
        total = total + lax.ppermute(sent, "tensor", _pairs(lambda t, k=k: t + 4 * k)).astype(jnp.float32)
    mine = jnp.take(total, zh, axis=0)
    theirs = jnp.take(total, 1 - zh, axis=0).astype(jnp.bfloat16)
    return mine + lax.ppermute(theirs, "tensor", _pairs(lambda t: t ^ 2)).astype(jnp.float32)


def psum_tensor_f32(values):
    values = values + lax.ppermute(values, "tensor", _pairs(lambda t: t ^ 1))
    values = values + lax.ppermute(values, "tensor", _pairs(lambda t: t ^ 2))
    shifted = [lax.ppermute(values, "tensor", _pairs(lambda t, k=k: t + 4 * k)) for k in (1, 2, 3)]
    return values + shifted[0] + shifted[1] + shifted[2]


def slot_plan(lengths, prefix_id, placement_perm, group_index):
    requests = lax.dynamic_slice(placement_perm, (group_index * REQ_GRP,), (REQ_GRP,))
    req_sizes = jnp.take(lengths, requests)
    starts = jnp.cumsum(req_sizes) - req_sizes
    slot_ids = jnp.arange(CAP, dtype=jnp.int32)
    inside = (
        (slot_ids[None, :] >= starts[:, None]) & (slot_ids[None, :] < (starts + req_sizes)[:, None])
    ).astype(jnp.int32)
    live_slots = jnp.sum(inside, axis=0) > 0
    numbers = jnp.arange(1, REQ_GRP + 1, dtype=jnp.int32)
    owner_req = jnp.sum(inside * numbers[:, None], axis=0) - 1
    offsets = slot_ids - jnp.sum(inside * starts[:, None], axis=0)
    prefix_pick = jnp.sum(inside * jnp.take(prefix_id, requests)[:, None], axis=0)
    return (slot_ids, live_slots, owner_req, offsets, prefix_pick)


def rotate(values, offsets):
    half_dim = HD // 2
    inverse = jnp.power(ROPE_BASE, -2.0 * jnp.arange(half_dim, dtype=jnp.float32) / HD)
    angles = (offsets.astype(jnp.float32) + PLEN)[:, None] * inverse[None, :]
    cosine = jnp.cos(angles)[:, None, :]
    sine_part = jnp.sin(angles)[:, None, :]
    front_half = values[..., :half_dim]
    back_half = values[..., half_dim:]
    return jnp.concatenate(
        [front_half * cosine - back_half * sine_part, back_half * cosine + front_half * sine_part],
        axis=-1,
    )


def rms_scale(values, gain):
    mean_square = jnp.mean(values * values, axis=-1, keepdims=True)
    return values * lax.rsqrt(mean_square + EPSILON) * gain


def partial_softmax(scores, value_heads):
    running_max = jnp.max(scores, axis=-1, keepdims=True)
    weights = jnp.exp(scores - running_max)
    weight_sum = jnp.sum(weights, axis=-1, keepdims=True)
    accumulated = jnp.einsum(
        "hck,khd->hcd",
        weights.astype(jnp.bfloat16),
        value_heads,
        preferred_element_type=jnp.float32,
    )
    return (running_max, weight_sum, accumulated)


def merge_partials(partials):
    running_max = partials[0][0]
    for member in partials[1:]:
        running_max = jnp.maximum(running_max, member[0])
    weight_sum = jnp.zeros_like(partials[0][1])
    accumulated = jnp.zeros_like(partials[0][2])
    for member in partials:
        factor = jnp.exp(member[0] - running_max)
        weight_sum = weight_sum + factor * member[1]
        accumulated = accumulated + factor * member[2]
    return accumulated / weight_sum


def body(
    hidden,
    lengths,
    prefix_id,
    placement_perm,
    prefix_owner,
    prefix_cache,
    qkv_weight,
    q_gain,
    k_gain,
    out_weight,
    attn_gain,
    gate_up_weight,
    down_weight,
    mlp_gain,
):
    tensor_rank = lax.axis_index("tensor")
    group_index = lax.axis_index("dp")
    slot_ids, live_slots, owner_req, offsets, prefix_pick = slot_plan(
        lengths, prefix_id, placement_perm, group_index
    )
    local_rows = hidden.shape[0]
    local_width = qkv_weight.shape[2]
    local_heads = local_width // HD
    row_start = tensor_rank * local_rows
    column_start = tensor_rank * local_width
    score_scale = HD ** (-0.5)
    full_rows = ag_tensor(hidden)
    projected = jnp.einsum("cd,kde->kce", full_rows, qkv_weight, preferred_element_type=jnp.float32)
    norm_gains = jnp.stack(
        [
            lax.dynamic_slice_in_dim(q_gain, column_start, local_width),
            lax.dynamic_slice_in_dim(k_gain, column_start, local_width),
        ]
    )
    squares = jnp.sum(projected[:2] * projected[:2], axis=2)
    totals = psum_tensor_f32(squares)
    normed = projected[:2] * lax.rsqrt(totals / D + EPSILON)[:, :, None] * norm_gains[:, None, :]
    queries = rotate(normed[0].reshape(CAP, local_heads, HD), offsets).astype(jnp.bfloat16)
    key_heads = rotate(normed[1].reshape(CAP, local_heads, HD), offsets).astype(jnp.bfloat16)
    value_heads = projected[2].astype(jnp.bfloat16).reshape(CAP, local_heads, HD)
    suf_scores = (
        jnp.einsum("chd,khd->hck", queries, key_heads, preferred_element_type=jnp.float32)
        * score_scale
    )
    visible = (
        (owner_req[:, None] == owner_req[None, :])
        & live_slots[None, :]
        & (slot_ids[None, :] <= slot_ids[:, None])
    )
    suf_scores = jnp.where(visible[None], suf_scores, MASKED_SCORE)
    partials = [partial_softmax(suf_scores, value_heads)]
    for prefix_num in range(2):
        prefix_kv = from_root(prefix_cache[0], "dp", prefix_owner[prefix_num])
        prefix_keys = prefix_kv[0].reshape(PLEN, local_heads, HD)
        prefix_values = prefix_kv[1].reshape(PLEN, local_heads, HD)
        pre_scores = (
            jnp.einsum("chd,khd->hck", queries, prefix_keys, preferred_element_type=jnp.float32)
            * score_scale
        )
        pre_scores = jnp.where((prefix_pick == prefix_num)[None, :, None], pre_scores, MASKED_SCORE)
        partials.append(partial_softmax(pre_scores, prefix_values))
    attended = merge_partials(partials).astype(jnp.bfloat16)
    attended = attended.transpose(1, 0, 2).reshape(CAP, local_width)
    summed = rs_tensor(
        jnp.dot(attended, out_weight, preferred_element_type=jnp.float32).astype(jnp.bfloat16)
    )
    mid_rows = (hidden.astype(jnp.float32) + rms_scale(summed, attn_gain)).astype(jnp.bfloat16)
    merged = ag_tensor(mid_rows)
    gate_up = jnp.einsum("cd,kdf->kcf", merged, gate_up_weight, preferred_element_type=jnp.float32)
    activated = (jax.nn.silu(gate_up[0]) * gate_up[1]).astype(jnp.bfloat16)
    mlp_term = rs_tensor(
        jnp.dot(activated, down_weight, preferred_element_type=jnp.float32).astype(jnp.bfloat16)
    )
    result = mid_rows.astype(jnp.float32) + rms_scale(mlp_term, mlp_gain)
    live_rows = lax.dynamic_slice_in_dim(live_slots, row_start, local_rows, 0)
    hidden_out = jnp.where(live_rows[:, None], result, 0.0).astype(jnp.bfloat16)
    key_out = jnp.where(live_slots[:, None], key_heads.reshape(CAP, local_width), 0.0)
    value_out = jnp.where(live_slots[:, None], value_heads.reshape(CAP, local_width), 0.0)
    suffix_kv = jnp.stack([key_out, value_out])
    return (hidden_out, suffix_kv)


def solution(mesh):
    in_specs = (
        P(("dp", "tensor"), None),
        P(),
        P(),
        P(),
        P(),
        P("dp", None, None, "tensor"),
        P(None, None, "tensor"),
        P(),
        P(),
        P("tensor", None),
        P(),
        P(None, None, "tensor"),
        P("tensor", None),
        P(),
    )
    out_specs = (P(("dp", "tensor"), None), P(None, "dp", "tensor"))
    return jax.shard_map(body, mesh=mesh, in_specs=in_specs, out_specs=out_specs, check_vma=False)
```

```python
import jax
import jax.numpy as jnp
from jax import lax
from jax.sharding import PartitionSpec as P

D = 2048
HD = 128
CAP = 768
REQ_GRP = 4
PLEN = 4096


ROPE_BASE = 500000.0
EPSILON = 1e-06
MASKED_SCORE = -1e30


def from_root(shard, axis, root):
    mine = lax.axis_index(axis) == root
    return lax.psum(jnp.where(mine, shard, jnp.zeros_like(shard)), axis)


def _pairs(fn, n=16):
    return [(t, fn(t) % n) for t in range(n)]


def tensor_coords():
    t = lax.axis_index("tensor")
    return t // 4, (t // 2) % 2, t % 2


def ag_tensor(block):
    x_i, zh, c = tensor_coords()
    other = lax.ppermute(block, "tensor", _pairs(lambda t: t ^ 2))
    pair = jnp.where(zh == 0, jnp.stack([block, other]), jnp.stack([other, block]))
    from_x = [lax.ppermute(pair, "tensor", _pairs(lambda t, k=k: t + 4 * k)) for k in (3, 2, 1)]
    quad = jnp.roll(jnp.stack([pair] + from_x), x_i, axis=0)
    mate = lax.ppermute(quad, "tensor", _pairs(lambda t: t ^ 1))
    full = jnp.where(c == 0, jnp.stack([quad, mate], axis=2), jnp.stack([mate, quad], axis=2))
    return full.reshape((-1,) + block.shape[1:])


def rs_tensor(rows):
    x_i, zh, c = tensor_coords()
    grid = rows.reshape((4, 2, 2, -1) + rows.shape[1:])
    mine = jnp.take(grid, c, axis=2).astype(jnp.float32)
    theirs = jnp.take(grid, 1 - c, axis=2).astype(jnp.bfloat16)
    summed = mine + lax.ppermute(theirs, "tensor", _pairs(lambda t: t ^ 1)).astype(jnp.float32)
    rel = jnp.roll(summed, -x_i, axis=0)
    total = rel[0]
    for k in (1, 2, 3):
        sent = rel[k].astype(jnp.bfloat16)
        total = total + lax.ppermute(sent, "tensor", _pairs(lambda t, k=k: t + 4 * k)).astype(jnp.float32)
    mine = jnp.take(total, zh, axis=0)
    theirs = jnp.take(total, 1 - zh, axis=0).astype(jnp.bfloat16)
    return mine + lax.ppermute(theirs, "tensor", _pairs(lambda t: t ^ 2)).astype(jnp.float32)


def psum_tensor_f32(values):
    values = values + lax.ppermute(values, "tensor", _pairs(lambda t: t ^ 1))
    values = values + lax.ppermute(values, "tensor", _pairs(lambda t: t ^ 2))
    shifted = [lax.ppermute(values, "tensor", _pairs(lambda t, k=k: t + 4 * k)) for k in (1, 2, 3)]
    return values + shifted[0] + shifted[1] + shifted[2]


def fetch_prefixes(own_slot, prefix_owner):
    n_dp = lax.axis_size("dp")
    g = lax.axis_index("dp")
    piece = own_slot.shape[1] // n_dp
    received = [lax.dynamic_slice_in_dim(own_slot, g * piece, piece, axis=1)]
    for k in range(1, n_dp):
        sent = lax.dynamic_slice_in_dim(own_slot, ((g - k) % n_dp) * piece, piece, axis=1)
        received.append(lax.ppermute(sent, "dp", _pairs(lambda i, k=k: i - k, n_dp)))
    by_shift = jnp.stack(received)
    mine = jnp.stack([jnp.take(by_shift, (prefix_owner[p] - g) % n_dp, axis=0) for p in range(2)])
    gathered = [mine] + [
        lax.ppermute(mine, "dp", _pairs(lambda i, k=k: i - k, n_dp)) for k in range(1, n_dp)
    ]
    ordered = jnp.roll(jnp.stack(gathered), g, axis=0)
    ordered = jnp.moveaxis(ordered, 0, 2)
    return ordered.reshape(ordered.shape[:2] + (-1,) + ordered.shape[4:])


def slot_plan(lengths, prefix_id, placement_perm, group_index):
    requests = lax.dynamic_slice(placement_perm, (group_index * REQ_GRP,), (REQ_GRP,))
    req_sizes = jnp.take(lengths, requests)
    starts = jnp.cumsum(req_sizes) - req_sizes
    slot_ids = jnp.arange(CAP, dtype=jnp.int32)
    inside = (
        (slot_ids[None, :] >= starts[:, None]) & (slot_ids[None, :] < (starts + req_sizes)[:, None])
    ).astype(jnp.int32)
    live_slots = jnp.sum(inside, axis=0) > 0
    numbers = jnp.arange(1, REQ_GRP + 1, dtype=jnp.int32)
    owner_req = jnp.sum(inside * numbers[:, None], axis=0) - 1
    offsets = slot_ids - jnp.sum(inside * starts[:, None], axis=0)
    prefix_pick = jnp.sum(inside * jnp.take(prefix_id, requests)[:, None], axis=0)
    return (slot_ids, live_slots, owner_req, offsets, prefix_pick)


def rotate(values, offsets):
    half_dim = HD // 2
    inverse = jnp.power(ROPE_BASE, -2.0 * jnp.arange(half_dim, dtype=jnp.float32) / HD)
    angles = (offsets.astype(jnp.float32) + PLEN)[:, None] * inverse[None, :]
    cosine = jnp.cos(angles)[:, None, :]
    sine_part = jnp.sin(angles)[:, None, :]
    front_half = values[..., :half_dim]
    back_half = values[..., half_dim:]
    return jnp.concatenate(
        [front_half * cosine - back_half * sine_part, back_half * cosine + front_half * sine_part],
        axis=-1,
    )


def rms_scale(values, gain):
    mean_square = jnp.mean(values * values, axis=-1, keepdims=True)
    return values * lax.rsqrt(mean_square + EPSILON) * gain


def partial_softmax(scores, value_heads):
    running_max = jnp.max(scores, axis=-1, keepdims=True)
    weights = jnp.exp(scores - running_max)
    weight_sum = jnp.sum(weights, axis=-1, keepdims=True)
    accumulated = jnp.einsum(
        "hck,khd->hcd",
        weights.astype(jnp.bfloat16),
        value_heads,
        preferred_element_type=jnp.float32,
    )
    return (running_max, weight_sum, accumulated)


def merge_partials(partials):
    running_max = partials[0][0]
    for member in partials[1:]:
        running_max = jnp.maximum(running_max, member[0])
    weight_sum = jnp.zeros_like(partials[0][1])
    accumulated = jnp.zeros_like(partials[0][2])
    for member in partials:
        factor = jnp.exp(member[0] - running_max)
        weight_sum = weight_sum + factor * member[1]
        accumulated = accumulated + factor * member[2]
    return accumulated / weight_sum


def body(
    hidden,
    lengths,
    prefix_id,
    placement_perm,
    prefix_owner,
    prefix_cache,
    qkv_weight,
    q_gain,
    k_gain,
    out_weight,
    attn_gain,
    gate_up_weight,
    down_weight,
    mlp_gain,
):
    tensor_rank = lax.axis_index("tensor")
    group_index = lax.axis_index("dp")
    slot_ids, live_slots, owner_req, offsets, prefix_pick = slot_plan(
        lengths, prefix_id, placement_perm, group_index
    )
    local_rows = hidden.shape[0]
    local_width = qkv_weight.shape[2]
    local_heads = local_width // HD
    row_start = tensor_rank * local_rows
    column_start = tensor_rank * local_width
    score_scale = HD ** (-0.5)
    full_rows = ag_tensor(hidden)
    projected = jnp.einsum("cd,kde->kce", full_rows, qkv_weight, preferred_element_type=jnp.float32)
    norm_gains = jnp.stack(
        [
            lax.dynamic_slice_in_dim(q_gain, column_start, local_width),
            lax.dynamic_slice_in_dim(k_gain, column_start, local_width),
        ]
    )
    squares = jnp.sum(projected[:2] * projected[:2], axis=2)
    totals = psum_tensor_f32(squares)
    normed = projected[:2] * lax.rsqrt(totals / D + EPSILON)[:, :, None] * norm_gains[:, None, :]
    queries = rotate(normed[0].reshape(CAP, local_heads, HD), offsets).astype(jnp.bfloat16)
    key_heads = rotate(normed[1].reshape(CAP, local_heads, HD), offsets).astype(jnp.bfloat16)
    value_heads = projected[2].astype(jnp.bfloat16).reshape(CAP, local_heads, HD)
    suf_scores = (
        jnp.einsum("chd,khd->hck", queries, key_heads, preferred_element_type=jnp.float32)
        * score_scale
    )
    visible = (
        (owner_req[:, None] == owner_req[None, :])
        & live_slots[None, :]
        & (slot_ids[None, :] <= slot_ids[:, None])
    )
    suf_scores = jnp.where(visible[None], suf_scores, MASKED_SCORE)
    partials = [partial_softmax(suf_scores, value_heads)]
    both_prefixes = fetch_prefixes(prefix_cache[0], prefix_owner)
    for prefix_num in range(2):
        prefix_kv = both_prefixes[prefix_num]
        prefix_keys = prefix_kv[0].reshape(PLEN, local_heads, HD)
        prefix_values = prefix_kv[1].reshape(PLEN, local_heads, HD)
        pre_scores = (
            jnp.einsum("chd,khd->hck", queries, prefix_keys, preferred_element_type=jnp.float32)
            * score_scale
        )
        pre_scores = jnp.where((prefix_pick == prefix_num)[None, :, None], pre_scores, MASKED_SCORE)
        partials.append(partial_softmax(pre_scores, prefix_values))
    attended = merge_partials(partials).astype(jnp.bfloat16)
    attended = attended.transpose(1, 0, 2).reshape(CAP, local_width)
    summed = rs_tensor(
        jnp.dot(attended, out_weight, preferred_element_type=jnp.float32).astype(jnp.bfloat16)
    )
    mid_rows = (hidden.astype(jnp.float32) + rms_scale(summed, attn_gain)).astype(jnp.bfloat16)
    merged = ag_tensor(mid_rows)
    gate_up = jnp.einsum("cd,kdf->kcf", merged, gate_up_weight, preferred_element_type=jnp.float32)
    activated = (jax.nn.silu(gate_up[0]) * gate_up[1]).astype(jnp.bfloat16)
    mlp_term = rs_tensor(
        jnp.dot(activated, down_weight, preferred_element_type=jnp.float32).astype(jnp.bfloat16)
    )
    result = mid_rows.astype(jnp.float32) + rms_scale(mlp_term, mlp_gain)
    live_rows = lax.dynamic_slice_in_dim(live_slots, row_start, local_rows, 0)
    hidden_out = jnp.where(live_rows[:, None], result, 0.0).astype(jnp.bfloat16)
    key_out = jnp.where(live_slots[:, None], key_heads.reshape(CAP, local_width), 0.0)
    value_out = jnp.where(live_slots[:, None], value_heads.reshape(CAP, local_width), 0.0)
    suffix_kv = jnp.stack([key_out, value_out])
    return (hidden_out, suffix_kv)


def solution(mesh):
    in_specs = (
        P(("dp", "tensor"), None),
        P(),
        P(),
        P(),
        P(),
        P("dp", None, None, "tensor"),
        P(None, None, "tensor"),
        P(),
        P(),
        P("tensor", None),
        P(),
        P(None, None, "tensor"),
        P("tensor", None),
        P(),
    )
    out_specs = (P(("dp", "tensor"), None), P(None, "dp", "tensor"))
    return jax.shard_map(body, mesh=mesh, in_specs=in_specs, out_specs=out_specs, check_vma=False)
```

```python
import jax
import jax.numpy as jnp
from jax import lax
from jax.sharding import PartitionSpec as P

D = 2048
HD = 128
CAP = 768
REQ_GRP = 4
PLEN = 4096


ROPE_BASE = 500000.0
EPSILON = 1e-06
MASKED_SCORE = -1e30


def from_root(shard, axis, root):
    mine = lax.axis_index(axis) == root
    return lax.psum(jnp.where(mine, shard, jnp.zeros_like(shard)), axis)


def _pairs(fn, n=16):
    return [(t, fn(t) % n) for t in range(n)]


def tensor_coords():
    t = lax.axis_index("tensor")
    return t // 4, (t // 2) % 2, t % 2


def ag_tensor(block):
    x_i, zh, c = tensor_coords()
    other = lax.ppermute(block, "tensor", _pairs(lambda t: t ^ 2))
    pair = jnp.where(zh == 0, jnp.stack([block, other]), jnp.stack([other, block]))
    from_x = [lax.ppermute(pair, "tensor", _pairs(lambda t, k=k: t + 4 * k)) for k in (3, 2, 1)]
    quad = jnp.roll(jnp.stack([pair] + from_x), x_i, axis=0)
    mate = lax.ppermute(quad, "tensor", _pairs(lambda t: t ^ 1))
    full = jnp.where(c == 0, jnp.stack([quad, mate], axis=2), jnp.stack([mate, quad], axis=2))
    return full.reshape((-1,) + block.shape[1:])


def rs_tensor(rows):
    x_i, zh, c = tensor_coords()
    grid = rows.reshape((4, 2, 2, -1) + rows.shape[1:])
    mine = jnp.take(grid, c, axis=2).astype(jnp.float32)
    theirs = jnp.take(grid, 1 - c, axis=2).astype(jnp.bfloat16)
    summed = mine + lax.ppermute(theirs, "tensor", _pairs(lambda t: t ^ 1)).astype(jnp.float32)
    rel = jnp.roll(summed, -x_i, axis=0)
    total = rel[0]
    for k in (1, 2, 3):
        sent = rel[k].astype(jnp.bfloat16)
        total = total + lax.ppermute(sent, "tensor", _pairs(lambda t, k=k: t + 4 * k)).astype(jnp.float32)
    mine = jnp.take(total, zh, axis=0)
    theirs = jnp.take(total, 1 - zh, axis=0).astype(jnp.bfloat16)
    return mine + lax.ppermute(theirs, "tensor", _pairs(lambda t: t ^ 2)).astype(jnp.float32)


def psum_tensor_f32(values):
    values = values + lax.ppermute(values, "tensor", _pairs(lambda t: t ^ 1))
    values = values + lax.ppermute(values, "tensor", _pairs(lambda t: t ^ 2))
    shifted = [lax.ppermute(values, "tensor", _pairs(lambda t, k=k: t + 4 * k)) for k in (1, 2, 3)]
    return values + shifted[0] + shifted[1] + shifted[2]


def fetch_prefixes(own_slot, prefix_owner):
    g = lax.axis_index("dp")
    zl, y = g // 4, g % 4
    cols = own_slot.reshape((own_slot.shape[0], 4, 4, -1) + own_slot.shape[2:])
    by_col = [jnp.take(cols, y, axis=2)]
    for k in (1, 2, 3):
        sent = jnp.take(cols, (y + k) % 4, axis=2)
        pairs = _pairs(lambda i, k=k: (i // 4) * 4 + (i % 4 + k) % 4)
        by_col.append(lax.ppermute(sent, "dp", pairs))
    by_col = jnp.stack(by_col)
    rows = jnp.stack([jnp.take(by_col, (y - prefix_owner[p] % 4) % 4, axis=0) for p in range(2)])
    by_row = [jnp.take(rows, zl, axis=2)]
    for k in (1, 2, 3):
        sent = jnp.take(rows, (zl + k) % 4, axis=2)
        pairs = _pairs(lambda i, k=k: ((i // 4 + k) % 4) * 4 + i % 4)
        by_row.append(lax.ppermute(sent, "dp", pairs))
    by_row = jnp.stack(by_row)
    mine = jnp.stack(
        [jnp.take(by_row, (zl - prefix_owner[p] // 4) % 4, axis=0)[p] for p in range(2)]
    )
    gathered = lax.all_gather(mine, "dp", axis=2, tiled=False)
    return gathered.reshape(gathered.shape[:2] + (-1,) + gathered.shape[4:])


def slot_plan(lengths, prefix_id, placement_perm, group_index):
    requests = lax.dynamic_slice(placement_perm, (group_index * REQ_GRP,), (REQ_GRP,))
    req_sizes = jnp.take(lengths, requests)
    starts = jnp.cumsum(req_sizes) - req_sizes
    slot_ids = jnp.arange(CAP, dtype=jnp.int32)
    inside = (
        (slot_ids[None, :] >= starts[:, None]) & (slot_ids[None, :] < (starts + req_sizes)[:, None])
    ).astype(jnp.int32)
    live_slots = jnp.sum(inside, axis=0) > 0
    numbers = jnp.arange(1, REQ_GRP + 1, dtype=jnp.int32)
    owner_req = jnp.sum(inside * numbers[:, None], axis=0) - 1
    offsets = slot_ids - jnp.sum(inside * starts[:, None], axis=0)
    prefix_pick = jnp.sum(inside * jnp.take(prefix_id, requests)[:, None], axis=0)
    return (slot_ids, live_slots, owner_req, offsets, prefix_pick)


def rotate(values, offsets):
    half_dim = HD // 2
    inverse = jnp.power(ROPE_BASE, -2.0 * jnp.arange(half_dim, dtype=jnp.float32) / HD)
    angles = (offsets.astype(jnp.float32) + PLEN)[:, None] * inverse[None, :]
    cosine = jnp.cos(angles)[:, None, :]
    sine_part = jnp.sin(angles)[:, None, :]
    front_half = values[..., :half_dim]
    back_half = values[..., half_dim:]
    return jnp.concatenate(
        [front_half * cosine - back_half * sine_part, back_half * cosine + front_half * sine_part],
        axis=-1,
    )


def rms_scale(values, gain):
    mean_square = jnp.mean(values * values, axis=-1, keepdims=True)
    return values * lax.rsqrt(mean_square + EPSILON) * gain


def partial_softmax(scores, value_heads):
    running_max = jnp.max(scores, axis=-1, keepdims=True)
    weights = jnp.exp(scores - running_max)
    weight_sum = jnp.sum(weights, axis=-1, keepdims=True)
    accumulated = jnp.einsum(
        "hck,khd->hcd",
        weights.astype(jnp.bfloat16),
        value_heads,
        preferred_element_type=jnp.float32,
    )
    return (running_max, weight_sum, accumulated)


def merge_partials(partials):
    running_max = partials[0][0]
    for member in partials[1:]:
        running_max = jnp.maximum(running_max, member[0])
    weight_sum = jnp.zeros_like(partials[0][1])
    accumulated = jnp.zeros_like(partials[0][2])
    for member in partials:
        factor = jnp.exp(member[0] - running_max)
        weight_sum = weight_sum + factor * member[1]
        accumulated = accumulated + factor * member[2]
    return accumulated / weight_sum


def body(
    hidden,
    lengths,
    prefix_id,
    placement_perm,
    prefix_owner,
    prefix_cache,
    qkv_weight,
    q_gain,
    k_gain,
    out_weight,
    attn_gain,
    gate_up_weight,
    down_weight,
    mlp_gain,
):
    tensor_rank = lax.axis_index("tensor")
    group_index = lax.axis_index("dp")
    slot_ids, live_slots, owner_req, offsets, prefix_pick = slot_plan(
        lengths, prefix_id, placement_perm, group_index
    )
    local_rows = hidden.shape[0]
    local_width = qkv_weight.shape[2]
    local_heads = local_width // HD
    row_start = tensor_rank * local_rows
    column_start = tensor_rank * local_width
    score_scale = HD ** (-0.5)
    full_rows = ag_tensor(hidden)
    projected = jnp.einsum("cd,kde->kce", full_rows, qkv_weight, preferred_element_type=jnp.float32)
    norm_gains = jnp.stack(
        [
            lax.dynamic_slice_in_dim(q_gain, column_start, local_width),
            lax.dynamic_slice_in_dim(k_gain, column_start, local_width),
        ]
    )
    squares = jnp.sum(projected[:2] * projected[:2], axis=2)
    totals = psum_tensor_f32(squares)
    normed = projected[:2] * lax.rsqrt(totals / D + EPSILON)[:, :, None] * norm_gains[:, None, :]
    queries = rotate(normed[0].reshape(CAP, local_heads, HD), offsets).astype(jnp.bfloat16)
    key_heads = rotate(normed[1].reshape(CAP, local_heads, HD), offsets).astype(jnp.bfloat16)
    value_heads = projected[2].astype(jnp.bfloat16).reshape(CAP, local_heads, HD)
    suf_scores = (
        jnp.einsum("chd,khd->hck", queries, key_heads, preferred_element_type=jnp.float32)
        * score_scale
    )
    visible = (
        (owner_req[:, None] == owner_req[None, :])
        & live_slots[None, :]
        & (slot_ids[None, :] <= slot_ids[:, None])
    )
    suf_scores = jnp.where(visible[None], suf_scores, MASKED_SCORE)
    partials = [partial_softmax(suf_scores, value_heads)]
    both_prefixes = fetch_prefixes(prefix_cache[0], prefix_owner)
    for prefix_num in range(2):
        prefix_kv = both_prefixes[prefix_num]
        prefix_keys = prefix_kv[0].reshape(PLEN, local_heads, HD)
        prefix_values = prefix_kv[1].reshape(PLEN, local_heads, HD)
        pre_scores = (
            jnp.einsum("chd,khd->hck", queries, prefix_keys, preferred_element_type=jnp.float32)
            * score_scale
        )
        pre_scores = jnp.where((prefix_pick == prefix_num)[None, :, None], pre_scores, MASKED_SCORE)
        partials.append(partial_softmax(pre_scores, prefix_values))
    attended = merge_partials(partials).astype(jnp.bfloat16)
    attended = attended.transpose(1, 0, 2).reshape(CAP, local_width)
    summed = rs_tensor(
        jnp.dot(attended, out_weight, preferred_element_type=jnp.float32).astype(jnp.bfloat16)
    )
    mid_rows = (hidden.astype(jnp.float32) + rms_scale(summed, attn_gain)).astype(jnp.bfloat16)
    merged = ag_tensor(mid_rows)
    gate_up = jnp.einsum("cd,kdf->kcf", merged, gate_up_weight, preferred_element_type=jnp.float32)
    activated = (jax.nn.silu(gate_up[0]) * gate_up[1]).astype(jnp.bfloat16)
    mlp_term = rs_tensor(
        jnp.dot(activated, down_weight, preferred_element_type=jnp.float32).astype(jnp.bfloat16)
    )
    result = mid_rows.astype(jnp.float32) + rms_scale(mlp_term, mlp_gain)
    live_rows = lax.dynamic_slice_in_dim(live_slots, row_start, local_rows, 0)
    hidden_out = jnp.where(live_rows[:, None], result, 0.0).astype(jnp.bfloat16)
    key_out = jnp.where(live_slots[:, None], key_heads.reshape(CAP, local_width), 0.0)
    value_out = jnp.where(live_slots[:, None], value_heads.reshape(CAP, local_width), 0.0)
    suffix_kv = jnp.stack([key_out, value_out])
    return (hidden_out, suffix_kv)


def solution(mesh):
    in_specs = (
        P(("dp", "tensor"), None),
        P(),
        P(),
        P(),
        P(),
        P("dp", None, None, "tensor"),
        P(None, None, "tensor"),
        P(),
        P(),
        P("tensor", None),
        P(),
        P(None, None, "tensor"),
        P("tensor", None),
        P(),
    )
    out_specs = (P(("dp", "tensor"), None), P(None, "dp", "tensor"))
    return jax.shard_map(body, mesh=mesh, in_specs=in_specs, out_specs=out_specs, check_vma=False)
```

```python
import jax
import jax.numpy as jnp
from jax import lax
from jax.sharding import PartitionSpec as P
from jax.experimental import pallas as pl
from jax.experimental.pallas import tpu as pltpu

D = 2048
HD = 128
CAP = 768
REQ_GRP = 4
PLEN = 4096


ROPE_BASE = 500000.0
EPSILON = 1e-06
MASKED_SCORE = -1e30


def from_root(shard, axis, root):
    mine = lax.axis_index(axis) == root
    return lax.psum(jnp.where(mine, shard, jnp.zeros_like(shard)), axis)


def _pairs(fn, n=16):
    return [(t, fn(t) % n) for t in range(n)]


def tensor_coords():
    t = lax.axis_index("tensor")
    return t // 4, (t // 2) % 2, t % 2


def ag_tensor(block):
    x_i, zh, c = tensor_coords()
    other = lax.ppermute(block, "tensor", _pairs(lambda t: t ^ 2))
    pair = jnp.where(zh == 0, jnp.stack([block, other]), jnp.stack([other, block]))
    from_x = [lax.ppermute(pair, "tensor", _pairs(lambda t, k=k: t + 4 * k)) for k in (3, 2, 1)]
    quad = jnp.roll(jnp.stack([pair] + from_x), x_i, axis=0)
    mate = lax.ppermute(quad, "tensor", _pairs(lambda t: t ^ 1))
    full = jnp.where(c == 0, jnp.stack([quad, mate], axis=2), jnp.stack([mate, quad], axis=2))
    return full.reshape((-1,) + block.shape[1:])


def rs_tensor(rows):
    x_i, zh, c = tensor_coords()
    grid = rows.reshape((4, 2, 2, -1) + rows.shape[1:])
    mine = jnp.take(grid, c, axis=2).astype(jnp.float32)
    theirs = jnp.take(grid, 1 - c, axis=2).astype(jnp.bfloat16)
    summed = mine + lax.ppermute(theirs, "tensor", _pairs(lambda t: t ^ 1)).astype(jnp.float32)
    rel = jnp.roll(summed, -x_i, axis=0)
    total = rel[0]
    for k in (1, 2, 3):
        sent = rel[k].astype(jnp.bfloat16)
        total = total + lax.ppermute(sent, "tensor", _pairs(lambda t, k=k: t + 4 * k)).astype(jnp.float32)
    mine = jnp.take(total, zh, axis=0)
    theirs = jnp.take(total, 1 - zh, axis=0).astype(jnp.bfloat16)
    return mine + lax.ppermute(theirs, "tensor", _pairs(lambda t: t ^ 2)).astype(jnp.float32)


def psum_tensor_f32(values):
    values = values + lax.ppermute(values, "tensor", _pairs(lambda t: t ^ 1))
    values = values + lax.ppermute(values, "tensor", _pairs(lambda t: t ^ 2))
    shifted = [lax.ppermute(values, "tensor", _pairs(lambda t, k=k: t + 4 * k)) for k in (1, 2, 3)]
    return values + shifted[0] + shifted[1] + shifted[2]


def fetch_prefixes(own_slot, prefix_owner):
    g = lax.axis_index("dp")
    zl, y = g // 4, g % 4
    cols = own_slot.reshape((own_slot.shape[0], 4, 4, -1) + own_slot.shape[2:])
    by_col = [jnp.take(cols, y, axis=2)]
    for k in (1, 2, 3):
        sent = jnp.take(cols, (y + k) % 4, axis=2)
        pairs = _pairs(lambda i, k=k: (i // 4) * 4 + (i % 4 + k) % 4)
        by_col.append(lax.ppermute(sent, "dp", pairs))
    by_col = jnp.stack(by_col)
    rows = jnp.stack([jnp.take(by_col, (y - prefix_owner[p] % 4) % 4, axis=0) for p in range(2)])
    by_row = [jnp.take(rows, zl, axis=2)]
    for k in (1, 2, 3):
        sent = jnp.take(rows, (zl + k) % 4, axis=2)
        pairs = _pairs(lambda i, k=k: ((i // 4 + k) % 4) * 4 + i % 4)
        by_row.append(lax.ppermute(sent, "dp", pairs))
    by_row = jnp.stack(by_row)
    mine = jnp.stack(
        [jnp.take(by_row, (zl - prefix_owner[p] // 4) % 4, axis=0)[p] for p in range(2)]
    )
    gathered = lax.all_gather(mine, "dp", axis=2, tiled=False)
    return gathered.reshape(gathered.shape[:2] + (-1,) + gathered.shape[4:])


def _prefix_kernel(pick_ref, q_ref, kv_ref, m_ref, l_ref, acc_ref):
    q = q_ref[...]
    dims = (((1,), (1,)), ((), ()))
    first = pick_ref[...] == 0
    s0 = lax.dot_general(q, kv_ref[0, 0], dims, preferred_element_type=jnp.float32)
    s1 = lax.dot_general(q, kv_ref[1, 0], dims, preferred_element_type=jnp.float32)
    scores = jnp.where(first, s0, s1) * (HD ** (-0.5))
    top = jnp.max(scores, axis=1, keepdims=True)
    weights = jnp.exp(scores - top)
    m_ref[...] = top
    l_ref[...] = jnp.sum(weights, axis=1, keepdims=True)
    rounded = weights.astype(jnp.bfloat16)
    a0 = jnp.dot(rounded, kv_ref[0, 1], preferred_element_type=jnp.float32)
    a1 = jnp.dot(rounded, kv_ref[1, 1], preferred_element_type=jnp.float32)
    acc_ref[...] = jnp.where(first, a0, a1)


def prefix_attention(queries, both_prefixes, prefix_pick, block=128):
    rows, width = queries.shape
    kv_shape = both_prefixes.shape
    col = pl.BlockSpec((block, 1), lambda i: (i, 0))
    return pl.pallas_call(
        _prefix_kernel,
        grid=(rows // block,),
        in_specs=[
            col,
            pl.BlockSpec((block, width), lambda i: (i, 0)),
            pl.BlockSpec(kv_shape, lambda i: (0, 0, 0, 0)),
        ],
        out_specs=[col, col, pl.BlockSpec((block, width), lambda i: (i, 0))],
        out_shape=[
            jax.ShapeDtypeStruct((rows, 1), jnp.float32),
            jax.ShapeDtypeStruct((rows, 1), jnp.float32),
            jax.ShapeDtypeStruct((rows, width), jnp.float32),
        ],
    )(prefix_pick.reshape(rows, 1).astype(jnp.int32), queries, both_prefixes)


def slot_plan(lengths, prefix_id, placement_perm, group_index):
    requests = lax.dynamic_slice(placement_perm, (group_index * REQ_GRP,), (REQ_GRP,))
    req_sizes = jnp.take(lengths, requests)
    starts = jnp.cumsum(req_sizes) - req_sizes
    slot_ids = jnp.arange(CAP, dtype=jnp.int32)
    inside = (
        (slot_ids[None, :] >= starts[:, None]) & (slot_ids[None, :] < (starts + req_sizes)[:, None])
    ).astype(jnp.int32)
    live_slots = jnp.sum(inside, axis=0) > 0
    numbers = jnp.arange(1, REQ_GRP + 1, dtype=jnp.int32)
    owner_req = jnp.sum(inside * numbers[:, None], axis=0) - 1
    offsets = slot_ids - jnp.sum(inside * starts[:, None], axis=0)
    prefix_pick = jnp.sum(inside * jnp.take(prefix_id, requests)[:, None], axis=0)
    return (slot_ids, live_slots, owner_req, offsets, prefix_pick)


def rotate(values, offsets):
    half_dim = HD // 2
    inverse = jnp.power(ROPE_BASE, -2.0 * jnp.arange(half_dim, dtype=jnp.float32) / HD)
    angles = (offsets.astype(jnp.float32) + PLEN)[:, None] * inverse[None, :]
    cosine = jnp.cos(angles)[:, None, :]
    sine_part = jnp.sin(angles)[:, None, :]
    front_half = values[..., :half_dim]
    back_half = values[..., half_dim:]
    return jnp.concatenate(
        [front_half * cosine - back_half * sine_part, back_half * cosine + front_half * sine_part],
        axis=-1,
    )


def rms_scale(values, gain):
    mean_square = jnp.mean(values * values, axis=-1, keepdims=True)
    return values * lax.rsqrt(mean_square + EPSILON) * gain


def partial_softmax(scores, value_heads):
    running_max = jnp.max(scores, axis=-1, keepdims=True)
    weights = jnp.exp(scores - running_max)
    weight_sum = jnp.sum(weights, axis=-1, keepdims=True)
    accumulated = jnp.einsum(
        "hck,khd->hcd",
        weights.astype(jnp.bfloat16),
        value_heads,
        preferred_element_type=jnp.float32,
    )
    return (running_max, weight_sum, accumulated)


def merge_partials(partials):
    running_max = partials[0][0]
    for member in partials[1:]:
        running_max = jnp.maximum(running_max, member[0])
    weight_sum = jnp.zeros_like(partials[0][1])
    accumulated = jnp.zeros_like(partials[0][2])
    for member in partials:
        factor = jnp.exp(member[0] - running_max)
        weight_sum = weight_sum + factor * member[1]
        accumulated = accumulated + factor * member[2]
    return accumulated / weight_sum


def body(
    hidden,
    lengths,
    prefix_id,
    placement_perm,
    prefix_owner,
    prefix_cache,
    qkv_weight,
    q_gain,
    k_gain,
    out_weight,
    attn_gain,
    gate_up_weight,
    down_weight,
    mlp_gain,
):
    tensor_rank = lax.axis_index("tensor")
    group_index = lax.axis_index("dp")
    slot_ids, live_slots, owner_req, offsets, prefix_pick = slot_plan(
        lengths, prefix_id, placement_perm, group_index
    )
    local_rows = hidden.shape[0]
    local_width = qkv_weight.shape[2]
    local_heads = local_width // HD
    assert local_heads == 1
    row_start = tensor_rank * local_rows
    column_start = tensor_rank * local_width
    score_scale = HD ** (-0.5)
    full_rows = ag_tensor(hidden)
    projected = jnp.einsum("cd,kde->kce", full_rows, qkv_weight, preferred_element_type=jnp.float32)
    norm_gains = jnp.stack(
        [
            lax.dynamic_slice_in_dim(q_gain, column_start, local_width),
            lax.dynamic_slice_in_dim(k_gain, column_start, local_width),
        ]
    )
    squares = jnp.sum(projected[:2] * projected[:2], axis=2)
    totals = psum_tensor_f32(squares)
    normed = projected[:2] * lax.rsqrt(totals / D + EPSILON)[:, :, None] * norm_gains[:, None, :]
    queries = rotate(normed[0].reshape(CAP, local_heads, HD), offsets).astype(jnp.bfloat16)
    key_heads = rotate(normed[1].reshape(CAP, local_heads, HD), offsets).astype(jnp.bfloat16)
    value_heads = projected[2].astype(jnp.bfloat16).reshape(CAP, local_heads, HD)
    suf_scores = (
        jnp.einsum("chd,khd->hck", queries, key_heads, preferred_element_type=jnp.float32)
        * score_scale
    )
    visible = (
        (owner_req[:, None] == owner_req[None, :])
        & live_slots[None, :]
        & (slot_ids[None, :] <= slot_ids[:, None])
    )
    suf_scores = jnp.where(visible[None], suf_scores, MASKED_SCORE)
    partials = [partial_softmax(suf_scores, value_heads)]
    both_prefixes = fetch_prefixes(prefix_cache[0], prefix_owner)
    top, total, acc = prefix_attention(queries.reshape(CAP, HD), both_prefixes, prefix_pick)
    partials.append((top[None], total[None], acc[None]))
    attended = merge_partials(partials).astype(jnp.bfloat16)
    attended = attended.transpose(1, 0, 2).reshape(CAP, local_width)
    summed = rs_tensor(
        jnp.dot(attended, out_weight, preferred_element_type=jnp.float32).astype(jnp.bfloat16)
    )
    mid_rows = (hidden.astype(jnp.float32) + rms_scale(summed, attn_gain)).astype(jnp.bfloat16)
    merged = ag_tensor(mid_rows)
    gate_up = jnp.einsum("cd,kdf->kcf", merged, gate_up_weight, preferred_element_type=jnp.float32)
    activated = (jax.nn.silu(gate_up[0]) * gate_up[1]).astype(jnp.bfloat16)
    mlp_term = rs_tensor(
        jnp.dot(activated, down_weight, preferred_element_type=jnp.float32).astype(jnp.bfloat16)
    )
    result = mid_rows.astype(jnp.float32) + rms_scale(mlp_term, mlp_gain)
    live_rows = lax.dynamic_slice_in_dim(live_slots, row_start, local_rows, 0)
    hidden_out = jnp.where(live_rows[:, None], result, 0.0).astype(jnp.bfloat16)
    key_out = jnp.where(live_slots[:, None], key_heads.reshape(CAP, local_width), 0.0)
    value_out = jnp.where(live_slots[:, None], value_heads.reshape(CAP, local_width), 0.0)
    suffix_kv = jnp.stack([key_out, value_out])
    return (hidden_out, suffix_kv)


def solution(mesh):
    in_specs = (
        P(("dp", "tensor"), None),
        P(),
        P(),
        P(),
        P(),
        P("dp", None, None, "tensor"),
        P(None, None, "tensor"),
        P(),
        P(),
        P("tensor", None),
        P(),
        P(None, None, "tensor"),
        P("tensor", None),
        P(),
    )
    out_specs = (P(("dp", "tensor"), None), P(None, "dp", "tensor"))
    return jax.shard_map(body, mesh=mesh, in_specs=in_specs, out_specs=out_specs, check_vma=False)
```

```python
import jax
import jax.numpy as jnp
from jax import lax
from jax.sharding import PartitionSpec as P
from jax.experimental import pallas as pl
from jax.experimental.pallas import tpu as pltpu

D = 2048
HD = 128
CAP = 768
REQ_GRP = 4
PLEN = 4096


ROPE_BASE = 500000.0
EPSILON = 1e-06
MASKED_SCORE = -1e30


def from_root(shard, axis, root):
    mine = lax.axis_index(axis) == root
    return lax.psum(jnp.where(mine, shard, jnp.zeros_like(shard)), axis)


def _pairs(fn, n=16):
    return [(t, fn(t) % n) for t in range(n)]


def tensor_coords():
    t = lax.axis_index("tensor")
    return t // 4, (t // 2) % 2, t % 2


def ag_tensor(block):
    x_i, zh, c = tensor_coords()
    other = lax.ppermute(block, "tensor", _pairs(lambda t: t ^ 2))
    pair = jnp.where(zh == 0, jnp.stack([block, other]), jnp.stack([other, block]))
    from_x = [lax.ppermute(pair, "tensor", _pairs(lambda t, k=k: t + 4 * k)) for k in (3, 2, 1)]
    quad = jnp.roll(jnp.stack([pair] + from_x), x_i, axis=0)
    mate = lax.ppermute(quad, "tensor", _pairs(lambda t: t ^ 1))
    full = jnp.where(c == 0, jnp.stack([quad, mate], axis=2), jnp.stack([mate, quad], axis=2))
    return full.reshape((-1,) + block.shape[1:])


def rs_tensor(rows):
    x_i, zh, c = tensor_coords()
    grid = rows.reshape((4, 2, 2, -1) + rows.shape[1:])
    mine = jnp.take(grid, c, axis=2).astype(jnp.float32)
    theirs = jnp.take(grid, 1 - c, axis=2).astype(jnp.bfloat16)
    summed = mine + lax.ppermute(theirs, "tensor", _pairs(lambda t: t ^ 1)).astype(jnp.float32)
    rel = jnp.roll(summed, -x_i, axis=0)
    total = rel[0]
    for k in (1, 2, 3):
        sent = rel[k].astype(jnp.bfloat16)
        total = total + lax.ppermute(sent, "tensor", _pairs(lambda t, k=k: t + 4 * k)).astype(jnp.float32)
    mine = jnp.take(total, zh, axis=0)
    theirs = jnp.take(total, 1 - zh, axis=0).astype(jnp.bfloat16)
    return mine + lax.ppermute(theirs, "tensor", _pairs(lambda t: t ^ 2)).astype(jnp.float32)


def psum_tensor_f32(values):
    values = values + lax.ppermute(values, "tensor", _pairs(lambda t: t ^ 1))
    values = values + lax.ppermute(values, "tensor", _pairs(lambda t: t ^ 2))
    shifted = [lax.ppermute(values, "tensor", _pairs(lambda t, k=k: t + 4 * k)) for k in (1, 2, 3)]
    return values + shifted[0] + shifted[1] + shifted[2]


def fetch_prefixes(own_slot, prefix_owner):
    g = lax.axis_index("dp")
    zl, y = g // 4, g % 4
    cols = own_slot.reshape((own_slot.shape[0], 4, 4, -1) + own_slot.shape[2:])
    by_col = [jnp.take(cols, y, axis=2)]
    for k in (1, 2, 3):
        sent = jnp.take(cols, (y + k) % 4, axis=2)
        pairs = _pairs(lambda i, k=k: (i // 4) * 4 + (i % 4 + k) % 4)
        by_col.append(lax.ppermute(sent, "dp", pairs))
    by_col = jnp.stack(by_col)
    rows = jnp.stack([jnp.take(by_col, (y - prefix_owner[p] % 4) % 4, axis=0) for p in range(2)])
    by_row = [jnp.take(rows, zl, axis=2)]
    for k in (1, 2, 3):
        sent = jnp.take(rows, (zl + k) % 4, axis=2)
        pairs = _pairs(lambda i, k=k: ((i // 4 + k) % 4) * 4 + i % 4)
        by_row.append(lax.ppermute(sent, "dp", pairs))
    by_row = jnp.stack(by_row)
    mine = jnp.stack(
        [jnp.take(by_row, (zl - prefix_owner[p] // 4) % 4, axis=0)[p] for p in range(2)]
    )
    keys = lax.all_gather(mine[:, 0], "dp", axis=1, tiled=True)
    values = lax.all_gather(jnp.swapaxes(mine[:, 1], 0, 1), "dp", axis=0, tiled=True)
    return jnp.stack([keys, jnp.swapaxes(values, 0, 1)], axis=1)


def _prefix_kernel(pick_ref, q_ref, kv_ref, m_ref, l_ref, acc_ref):
    q = q_ref[...]
    dims = (((1,), (1,)), ((), ()))
    first = pick_ref[...] == 0
    s0 = lax.dot_general(q, kv_ref[0, 0], dims, preferred_element_type=jnp.float32)
    s1 = lax.dot_general(q, kv_ref[1, 0], dims, preferred_element_type=jnp.float32)
    scores = jnp.where(first, s0, s1) * (HD ** (-0.5))
    top = jnp.max(scores, axis=1, keepdims=True)
    weights = jnp.exp(scores - top)
    m_ref[...] = top
    l_ref[...] = jnp.sum(weights, axis=1, keepdims=True)
    rounded = weights.astype(jnp.bfloat16)
    a0 = jnp.dot(rounded, kv_ref[0, 1], preferred_element_type=jnp.float32)
    a1 = jnp.dot(rounded, kv_ref[1, 1], preferred_element_type=jnp.float32)
    acc_ref[...] = jnp.where(first, a0, a1)


def prefix_attention(queries, both_prefixes, prefix_pick, block=128):
    rows, width = queries.shape
    kv_shape = both_prefixes.shape
    col = pl.BlockSpec((block, 1), lambda i: (i, 0))
    return pl.pallas_call(
        _prefix_kernel,
        grid=(rows // block,),
        in_specs=[
            col,
            pl.BlockSpec((block, width), lambda i: (i, 0)),
            pl.BlockSpec(kv_shape, lambda i: (0, 0, 0, 0)),
        ],
        out_specs=[col, col, pl.BlockSpec((block, width), lambda i: (i, 0))],
        out_shape=[
            jax.ShapeDtypeStruct((rows, 1), jnp.float32),
            jax.ShapeDtypeStruct((rows, 1), jnp.float32),
            jax.ShapeDtypeStruct((rows, width), jnp.float32),
        ],
    )(prefix_pick.reshape(rows, 1).astype(jnp.int32), queries, both_prefixes)


def slot_plan(lengths, prefix_id, placement_perm, group_index):
    requests = lax.dynamic_slice(placement_perm, (group_index * REQ_GRP,), (REQ_GRP,))
    req_sizes = jnp.take(lengths, requests)
    starts = jnp.cumsum(req_sizes) - req_sizes
    slot_ids = jnp.arange(CAP, dtype=jnp.int32)
    inside = (
        (slot_ids[None, :] >= starts[:, None]) & (slot_ids[None, :] < (starts + req_sizes)[:, None])
    ).astype(jnp.int32)
    live_slots = jnp.sum(inside, axis=0) > 0
    numbers = jnp.arange(1, REQ_GRP + 1, dtype=jnp.int32)
    owner_req = jnp.sum(inside * numbers[:, None], axis=0) - 1
    offsets = slot_ids - jnp.sum(inside * starts[:, None], axis=0)
    prefix_pick = jnp.sum(inside * jnp.take(prefix_id, requests)[:, None], axis=0)
    return (slot_ids, live_slots, owner_req, offsets, prefix_pick)


def rotate(values, offsets):
    half_dim = HD // 2
    inverse = jnp.power(ROPE_BASE, -2.0 * jnp.arange(half_dim, dtype=jnp.float32) / HD)
    angles = (offsets.astype(jnp.float32) + PLEN)[:, None] * inverse[None, :]
    cosine = jnp.cos(angles)[:, None, :]
    sine_part = jnp.sin(angles)[:, None, :]
    front_half = values[..., :half_dim]
    back_half = values[..., half_dim:]
    return jnp.concatenate(
        [front_half * cosine - back_half * sine_part, back_half * cosine + front_half * sine_part],
        axis=-1,
    )


def rms_scale(values, gain):
    mean_square = jnp.mean(values * values, axis=-1, keepdims=True)
    return values * lax.rsqrt(mean_square + EPSILON) * gain


def partial_softmax(scores, value_heads):
    running_max = jnp.max(scores, axis=-1, keepdims=True)
    weights = jnp.exp(scores - running_max)
    weight_sum = jnp.sum(weights, axis=-1, keepdims=True)
    accumulated = jnp.einsum(
        "hck,khd->hcd",
        weights.astype(jnp.bfloat16),
        value_heads,
        preferred_element_type=jnp.float32,
    )
    return (running_max, weight_sum, accumulated)


def merge_partials(partials):
    running_max = partials[0][0]
    for member in partials[1:]:
        running_max = jnp.maximum(running_max, member[0])
    weight_sum = jnp.zeros_like(partials[0][1])
    accumulated = jnp.zeros_like(partials[0][2])
    for member in partials:
        factor = jnp.exp(member[0] - running_max)
        weight_sum = weight_sum + factor * member[1]
        accumulated = accumulated + factor * member[2]
    return accumulated / weight_sum


def body(
    hidden,
    lengths,
    prefix_id,
    placement_perm,
    prefix_owner,
    prefix_cache,
    qkv_weight,
    q_gain,
    k_gain,
    out_weight,
    attn_gain,
    gate_up_weight,
    down_weight,
    mlp_gain,
):
    tensor_rank = lax.axis_index("tensor")
    group_index = lax.axis_index("dp")
    slot_ids, live_slots, owner_req, offsets, prefix_pick = slot_plan(
        lengths, prefix_id, placement_perm, group_index
    )
    local_rows = hidden.shape[0]
    local_width = qkv_weight.shape[2]
    local_heads = local_width // HD
    assert local_heads == 1
    row_start = tensor_rank * local_rows
    column_start = tensor_rank * local_width
    score_scale = HD ** (-0.5)
    full_rows = ag_tensor(hidden)
    projected = jnp.einsum("cd,kde->kce", full_rows, qkv_weight, preferred_element_type=jnp.float32)
    norm_gains = jnp.stack(
        [
            lax.dynamic_slice_in_dim(q_gain, column_start, local_width),
            lax.dynamic_slice_in_dim(k_gain, column_start, local_width),
        ]
    )
    squares = jnp.sum(projected[:2] * projected[:2], axis=2)
    totals = psum_tensor_f32(squares)
    normed = projected[:2] * lax.rsqrt(totals / D + EPSILON)[:, :, None] * norm_gains[:, None, :]
    queries = rotate(normed[0].reshape(CAP, local_heads, HD), offsets).astype(jnp.bfloat16)
    key_heads = rotate(normed[1].reshape(CAP, local_heads, HD), offsets).astype(jnp.bfloat16)
    value_heads = projected[2].astype(jnp.bfloat16).reshape(CAP, local_heads, HD)
    suf_scores = (
        jnp.einsum("chd,khd->hck", queries, key_heads, preferred_element_type=jnp.float32)
        * score_scale
    )
    visible = (
        (owner_req[:, None] == owner_req[None, :])
        & live_slots[None, :]
        & (slot_ids[None, :] <= slot_ids[:, None])
    )
    suf_scores = jnp.where(visible[None], suf_scores, MASKED_SCORE)
    partials = [partial_softmax(suf_scores, value_heads)]
    both_prefixes = fetch_prefixes(prefix_cache[0], prefix_owner)
    top, total, acc = prefix_attention(queries.reshape(CAP, HD), both_prefixes, prefix_pick)
    partials.append((top[None], total[None], acc[None]))
    attended = merge_partials(partials).astype(jnp.bfloat16)
    attended = attended.transpose(1, 0, 2).reshape(CAP, local_width)
    summed = rs_tensor(
        jnp.dot(attended, out_weight, preferred_element_type=jnp.float32).astype(jnp.bfloat16)
    )
    mid_rows = (hidden.astype(jnp.float32) + rms_scale(summed, attn_gain)).astype(jnp.bfloat16)
    merged = ag_tensor(mid_rows)
    gate_up = jnp.einsum("cd,kdf->kcf", merged, gate_up_weight, preferred_element_type=jnp.float32)
    activated = (jax.nn.silu(gate_up[0]) * gate_up[1]).astype(jnp.bfloat16)
    mlp_term = rs_tensor(
        jnp.dot(activated, down_weight, preferred_element_type=jnp.float32).astype(jnp.bfloat16)
    )
    result = mid_rows.astype(jnp.float32) + rms_scale(mlp_term, mlp_gain)
    live_rows = lax.dynamic_slice_in_dim(live_slots, row_start, local_rows, 0)
    hidden_out = jnp.where(live_rows[:, None], result, 0.0).astype(jnp.bfloat16)
    key_out = jnp.where(live_slots[:, None], key_heads.reshape(CAP, local_width), 0.0)
    value_out = jnp.where(live_slots[:, None], value_heads.reshape(CAP, local_width), 0.0)
    suffix_kv = jnp.stack([key_out, value_out])
    return (hidden_out, suffix_kv)


def solution(mesh):
    in_specs = (
        P(("dp", "tensor"), None),
        P(),
        P(),
        P(),
        P(),
        P("dp", None, None, "tensor"),
        P(None, None, "tensor"),
        P(),
        P(),
        P("tensor", None),
        P(),
        P(None, None, "tensor"),
        P("tensor", None),
        P(),
    )
    out_specs = (P(("dp", "tensor"), None), P(None, "dp", "tensor"))
    return jax.shard_map(body, mesh=mesh, in_specs=in_specs, out_specs=out_specs, check_vma=False)
```

```python
import jax
import jax.numpy as jnp
from jax import lax
from jax.sharding import PartitionSpec as P
from jax.experimental import pallas as pl
from jax.experimental.pallas import tpu as pltpu

D = 2048
HD = 128
CAP = 768
REQ_GRP = 4
PLEN = 4096


ROPE_BASE = 500000.0
EPSILON = 1e-06
MASKED_SCORE = -1e30


def from_root(shard, axis, root):
    mine = lax.axis_index(axis) == root
    return lax.psum(jnp.where(mine, shard, jnp.zeros_like(shard)), axis)


def _pairs(fn, n=16):
    return [(t, fn(t) % n) for t in range(n)]


def tensor_coords():
    t = lax.axis_index("tensor")
    return t // 4, (t // 2) % 2, t % 2


def ag_tensor(block):
    x_i, zh, c = tensor_coords()
    other = lax.ppermute(block, "tensor", _pairs(lambda t: t ^ 2))
    pair = jnp.where(zh == 0, jnp.stack([block, other]), jnp.stack([other, block]))
    from_x = [lax.ppermute(pair, "tensor", _pairs(lambda t, k=k: t + 4 * k)) for k in (3, 2, 1)]
    quad = jnp.roll(jnp.stack([pair] + from_x), x_i, axis=0)
    mate = lax.ppermute(quad, "tensor", _pairs(lambda t: t ^ 1))
    full = jnp.where(c == 0, jnp.stack([quad, mate], axis=2), jnp.stack([mate, quad], axis=2))
    return full.reshape((-1,) + block.shape[1:])


def rs_tensor(rows):
    x_i, zh, c = tensor_coords()
    grid = rows.reshape((4, 2, 2, -1) + rows.shape[1:])
    mine = jnp.take(grid, c, axis=2).astype(jnp.float32)
    theirs = jnp.take(grid, 1 - c, axis=2).astype(jnp.bfloat16)
    summed = mine + lax.ppermute(theirs, "tensor", _pairs(lambda t: t ^ 1)).astype(jnp.float32)
    rel = jnp.roll(summed, -x_i, axis=0)
    total = rel[0]
    for k in (1, 2, 3):
        sent = rel[k].astype(jnp.bfloat16)
        total = total + lax.ppermute(sent, "tensor", _pairs(lambda t, k=k: t + 4 * k)).astype(jnp.float32)
    mine = jnp.take(total, zh, axis=0)
    theirs = jnp.take(total, 1 - zh, axis=0).astype(jnp.bfloat16)
    return mine + lax.ppermute(theirs, "tensor", _pairs(lambda t: t ^ 2)).astype(jnp.float32)


def psum_tensor_f32(values):
    values = values + lax.ppermute(values, "tensor", _pairs(lambda t: t ^ 1))
    values = values + lax.ppermute(values, "tensor", _pairs(lambda t: t ^ 2))
    shifted = [lax.ppermute(values, "tensor", _pairs(lambda t, k=k: t + 4 * k)) for k in (1, 2, 3)]
    return values + shifted[0] + shifted[1] + shifted[2]


def fetch_prefixes(own_slot, prefix_owner):
    g = lax.axis_index("dp")
    zl, y = g // 4, g % 4
    cols = own_slot.reshape((own_slot.shape[0], 4, 4, -1) + own_slot.shape[2:])
    by_col = [jnp.take(cols, y, axis=2)]
    for k in (1, 2, 3):
        sent = jnp.take(cols, (y + k) % 4, axis=2)
        pairs = _pairs(lambda i, k=k: (i // 4) * 4 + (i % 4 + k) % 4)
        by_col.append(lax.ppermute(sent, "dp", pairs))
    by_col = jnp.stack(by_col)
    rows = jnp.stack([jnp.take(by_col, (y - prefix_owner[p] % 4) % 4, axis=0) for p in range(2)])
    by_row = [jnp.take(rows, zl, axis=2)]
    for k in (1, 2, 3):
        sent = jnp.take(rows, (zl + k) % 4, axis=2)
        pairs = _pairs(lambda i, k=k: ((i // 4 + k) % 4) * 4 + i % 4)
        by_row.append(lax.ppermute(sent, "dp", pairs))
    by_row = jnp.stack(by_row)
    mine = jnp.stack(
        [jnp.take(by_row, (zl - prefix_owner[p] // 4) % 4, axis=0)[p] for p in range(2)]
    )
    by_row = [mine]
    for k in (1, 2, 3):
        pairs = _pairs(lambda i, k=k: ((i // 4 - k) % 4) * 4 + i % 4)
        by_row.append(lax.ppermute(mine, "dp", pairs))
    column = jnp.roll(jnp.stack(by_row), zl, axis=0)
    by_col = [column]
    for k in (1, 2, 3):
        pairs = _pairs(lambda i, k=k: (i // 4) * 4 + (i % 4 - k) % 4)
        by_col.append(lax.ppermute(column, "dp", pairs))
    grid = jnp.roll(jnp.stack(by_col), y, axis=0)
    grid = jnp.transpose(grid, (2, 3, 1, 0, 4, 5))
    return grid.reshape(grid.shape[:2] + (-1,) + grid.shape[5:])


def _prefix_kernel(pick_ref, q_ref, kv_ref, m_ref, l_ref, acc_ref):
    q = q_ref[...]
    dims = (((1,), (1,)), ((), ()))
    first = pick_ref[...] == 0
    s0 = lax.dot_general(q, kv_ref[0, 0], dims, preferred_element_type=jnp.float32)
    s1 = lax.dot_general(q, kv_ref[1, 0], dims, preferred_element_type=jnp.float32)
    scores = jnp.where(first, s0, s1) * (HD ** (-0.5))
    top = jnp.max(scores, axis=1, keepdims=True)
    weights = jnp.exp(scores - top)
    m_ref[...] = top
    l_ref[...] = jnp.sum(weights, axis=1, keepdims=True)
    rounded = weights.astype(jnp.bfloat16)
    a0 = jnp.dot(rounded, kv_ref[0, 1], preferred_element_type=jnp.float32)
    a1 = jnp.dot(rounded, kv_ref[1, 1], preferred_element_type=jnp.float32)
    acc_ref[...] = jnp.where(first, a0, a1)


def prefix_attention(queries, both_prefixes, prefix_pick, block=128):
    rows, width = queries.shape
    kv_shape = both_prefixes.shape
    col = pl.BlockSpec((block, 1), lambda i: (i, 0))
    return pl.pallas_call(
        _prefix_kernel,
        grid=(rows // block,),
        in_specs=[
            col,
            pl.BlockSpec((block, width), lambda i: (i, 0)),
            pl.BlockSpec(kv_shape, lambda i: (0, 0, 0, 0)),
        ],
        out_specs=[col, col, pl.BlockSpec((block, width), lambda i: (i, 0))],
        out_shape=[
            jax.ShapeDtypeStruct((rows, 1), jnp.float32),
            jax.ShapeDtypeStruct((rows, 1), jnp.float32),
            jax.ShapeDtypeStruct((rows, width), jnp.float32),
        ],
    )(prefix_pick.reshape(rows, 1).astype(jnp.int32), queries, both_prefixes)


def slot_plan(lengths, prefix_id, placement_perm, group_index):
    requests = lax.dynamic_slice(placement_perm, (group_index * REQ_GRP,), (REQ_GRP,))
    req_sizes = jnp.take(lengths, requests)
    starts = jnp.cumsum(req_sizes) - req_sizes
    slot_ids = jnp.arange(CAP, dtype=jnp.int32)
    inside = (
        (slot_ids[None, :] >= starts[:, None]) & (slot_ids[None, :] < (starts + req_sizes)[:, None])
    ).astype(jnp.int32)
    live_slots = jnp.sum(inside, axis=0) > 0
    numbers = jnp.arange(1, REQ_GRP + 1, dtype=jnp.int32)
    owner_req = jnp.sum(inside * numbers[:, None], axis=0) - 1
    offsets = slot_ids - jnp.sum(inside * starts[:, None], axis=0)
    prefix_pick = jnp.sum(inside * jnp.take(prefix_id, requests)[:, None], axis=0)
    return (slot_ids, live_slots, owner_req, offsets, prefix_pick)


def rotate(values, offsets):
    half_dim = HD // 2
    inverse = jnp.power(ROPE_BASE, -2.0 * jnp.arange(half_dim, dtype=jnp.float32) / HD)
    angles = (offsets.astype(jnp.float32) + PLEN)[:, None] * inverse[None, :]
    cosine = jnp.cos(angles)[:, None, :]
    sine_part = jnp.sin(angles)[:, None, :]
    front_half = values[..., :half_dim]
    back_half = values[..., half_dim:]
    return jnp.concatenate(
        [front_half * cosine - back_half * sine_part, back_half * cosine + front_half * sine_part],
        axis=-1,
    )


def rms_scale(values, gain):
    mean_square = jnp.mean(values * values, axis=-1, keepdims=True)
    return values * lax.rsqrt(mean_square + EPSILON) * gain


def partial_softmax(scores, value_heads):
    running_max = jnp.max(scores, axis=-1, keepdims=True)
    weights = jnp.exp(scores - running_max)
    weight_sum = jnp.sum(weights, axis=-1, keepdims=True)
    accumulated = jnp.einsum(
        "hck,khd->hcd",
        weights.astype(jnp.bfloat16),
        value_heads,
        preferred_element_type=jnp.float32,
    )
    return (running_max, weight_sum, accumulated)


def merge_partials(partials):
    running_max = partials[0][0]
    for member in partials[1:]:
        running_max = jnp.maximum(running_max, member[0])
    weight_sum = jnp.zeros_like(partials[0][1])
    accumulated = jnp.zeros_like(partials[0][2])
    for member in partials:
        factor = jnp.exp(member[0] - running_max)
        weight_sum = weight_sum + factor * member[1]
        accumulated = accumulated + factor * member[2]
    return accumulated / weight_sum


def body(
    hidden,
    lengths,
    prefix_id,
    placement_perm,
    prefix_owner,
    prefix_cache,
    qkv_weight,
    q_gain,
    k_gain,
    out_weight,
    attn_gain,
    gate_up_weight,
    down_weight,
    mlp_gain,
):
    tensor_rank = lax.axis_index("tensor")
    group_index = lax.axis_index("dp")
    slot_ids, live_slots, owner_req, offsets, prefix_pick = slot_plan(
        lengths, prefix_id, placement_perm, group_index
    )
    local_rows = hidden.shape[0]
    local_width = qkv_weight.shape[2]
    local_heads = local_width // HD
    assert local_heads == 1
    row_start = tensor_rank * local_rows
    column_start = tensor_rank * local_width
    score_scale = HD ** (-0.5)
    full_rows = ag_tensor(hidden)
    projected = jnp.einsum("cd,kde->kce", full_rows, qkv_weight, preferred_element_type=jnp.float32)
    norm_gains = jnp.stack(
        [
            lax.dynamic_slice_in_dim(q_gain, column_start, local_width),
            lax.dynamic_slice_in_dim(k_gain, column_start, local_width),
        ]
    )
    squares = jnp.sum(projected[:2] * projected[:2], axis=2)
    totals = psum_tensor_f32(squares)
    normed = projected[:2] * lax.rsqrt(totals / D + EPSILON)[:, :, None] * norm_gains[:, None, :]
    queries = rotate(normed[0].reshape(CAP, local_heads, HD), offsets).astype(jnp.bfloat16)
    key_heads = rotate(normed[1].reshape(CAP, local_heads, HD), offsets).astype(jnp.bfloat16)
    value_heads = projected[2].astype(jnp.bfloat16).reshape(CAP, local_heads, HD)
    suf_scores = (
        jnp.einsum("chd,khd->hck", queries, key_heads, preferred_element_type=jnp.float32)
        * score_scale
    )
    visible = (
        (owner_req[:, None] == owner_req[None, :])
        & live_slots[None, :]
        & (slot_ids[None, :] <= slot_ids[:, None])
    )
    suf_scores = jnp.where(visible[None], suf_scores, MASKED_SCORE)
    partials = [partial_softmax(suf_scores, value_heads)]
    both_prefixes = fetch_prefixes(prefix_cache[0], prefix_owner)
    top, total, acc = prefix_attention(queries.reshape(CAP, HD), both_prefixes, prefix_pick)
    partials.append((top[None], total[None], acc[None]))
    attended = merge_partials(partials).astype(jnp.bfloat16)
    attended = attended.transpose(1, 0, 2).reshape(CAP, local_width)
    summed = rs_tensor(
        jnp.dot(attended, out_weight, preferred_element_type=jnp.float32).astype(jnp.bfloat16)
    )
    mid_rows = (hidden.astype(jnp.float32) + rms_scale(summed, attn_gain)).astype(jnp.bfloat16)
    merged = ag_tensor(mid_rows)
    gate_up = jnp.einsum("cd,kdf->kcf", merged, gate_up_weight, preferred_element_type=jnp.float32)
    activated = (jax.nn.silu(gate_up[0]) * gate_up[1]).astype(jnp.bfloat16)
    mlp_term = rs_tensor(
        jnp.dot(activated, down_weight, preferred_element_type=jnp.float32).astype(jnp.bfloat16)
    )
    result = mid_rows.astype(jnp.float32) + rms_scale(mlp_term, mlp_gain)
    live_rows = lax.dynamic_slice_in_dim(live_slots, row_start, local_rows, 0)
    hidden_out = jnp.where(live_rows[:, None], result, 0.0).astype(jnp.bfloat16)
    key_out = jnp.where(live_slots[:, None], key_heads.reshape(CAP, local_width), 0.0)
    value_out = jnp.where(live_slots[:, None], value_heads.reshape(CAP, local_width), 0.0)
    suffix_kv = jnp.stack([key_out, value_out])
    return (hidden_out, suffix_kv)


def solution(mesh):
    in_specs = (
        P(("dp", "tensor"), None),
        P(),
        P(),
        P(),
        P(),
        P("dp", None, None, "tensor"),
        P(None, None, "tensor"),
        P(),
        P(),
        P("tensor", None),
        P(),
        P(None, None, "tensor"),
        P("tensor", None),
        P(),
    )
    out_specs = (P(("dp", "tensor"), None), P(None, "dp", "tensor"))
    return jax.shard_map(body, mesh=mesh, in_specs=in_specs, out_specs=out_specs, check_vma=False)
```

```python
import jax
import jax.numpy as jnp
from jax import lax
from jax.sharding import PartitionSpec as P
from jax.experimental import pallas as pl
from jax.experimental.pallas import tpu as pltpu

D = 2048
HD = 128
CAP = 768
REQ_GRP = 4
PLEN = 4096


ROPE_BASE = 500000.0
EPSILON = 1e-06
MASKED_SCORE = -1e30


def from_root(shard, axis, root):
    mine = lax.axis_index(axis) == root
    return lax.psum(jnp.where(mine, shard, jnp.zeros_like(shard)), axis)


def _pairs(fn, n=16):
    return [(t, fn(t) % n) for t in range(n)]


def tensor_coords():
    t = lax.axis_index("tensor")
    return t // 4, (t // 2) % 2, t % 2


def ag_tensor(block):
    x_i, zh, c = tensor_coords()
    other = lax.ppermute(block, "tensor", _pairs(lambda t: t ^ 2))
    pair = jnp.where(zh == 0, jnp.stack([block, other]), jnp.stack([other, block]))
    from_x = [lax.ppermute(pair, "tensor", _pairs(lambda t, k=k: t + 4 * k)) for k in (3, 2, 1)]
    quad = jnp.roll(jnp.stack([pair] + from_x), x_i, axis=0)
    mate = lax.ppermute(quad, "tensor", _pairs(lambda t: t ^ 1))
    full = jnp.where(c == 0, jnp.stack([quad, mate], axis=2), jnp.stack([mate, quad], axis=2))
    return full.reshape((-1,) + block.shape[1:])


def rs_tensor(rows):
    x_i, zh, c = tensor_coords()
    grid = rows.reshape((4, 2, 2, -1) + rows.shape[1:])
    mine = jnp.take(grid, c, axis=2).astype(jnp.float32)
    theirs = jnp.take(grid, 1 - c, axis=2).astype(jnp.bfloat16)
    summed = mine + lax.ppermute(theirs, "tensor", _pairs(lambda t: t ^ 1)).astype(jnp.float32)
    rel = jnp.roll(summed, -x_i, axis=0)
    total = rel[0]
    for k in (1, 2, 3):
        sent = rel[k].astype(jnp.bfloat16)
        total = total + lax.ppermute(sent, "tensor", _pairs(lambda t, k=k: t + 4 * k)).astype(jnp.float32)
    mine = jnp.take(total, zh, axis=0)
    theirs = jnp.take(total, 1 - zh, axis=0).astype(jnp.bfloat16)
    return mine + lax.ppermute(theirs, "tensor", _pairs(lambda t: t ^ 2)).astype(jnp.float32)


def psum_tensor_f32(values):
    values = values + lax.ppermute(values, "tensor", _pairs(lambda t: t ^ 1))
    values = values + lax.ppermute(values, "tensor", _pairs(lambda t: t ^ 2))
    shifted = [lax.ppermute(values, "tensor", _pairs(lambda t, k=k: t + 4 * k)) for k in (1, 2, 3)]
    return values + shifted[0] + shifted[1] + shifted[2]


def fetch_prefixes(own_slot, prefix_owner, tied):
    g = lax.axis_index("dp")
    zl, y = g // 4, g % 4
    cols = own_slot.reshape((own_slot.shape[0], 4, 4, -1) + own_slot.shape[2:])
    by_col = [jnp.take(cols, y, axis=2)]
    for k in (1, 2, 3):
        sent = jnp.take(cols, (y + k) % 4, axis=2)
        pairs = _pairs(lambda i, k=k: (i // 4) * 4 + (i % 4 + k) % 4)
        by_col.append(lax.ppermute(sent, "dp", pairs))
    by_col = jnp.stack(by_col)
    rows = jnp.stack([jnp.take(by_col, (y - prefix_owner[p] % 4) % 4, axis=0) for p in range(2)])
    by_row = [jnp.take(rows, zl, axis=2)]
    for k in (1, 2, 3):
        sent = jnp.take(rows, (zl + k) % 4, axis=2)
        pairs = _pairs(lambda i, k=k: ((i // 4 + k) % 4) * 4 + i % 4)
        by_row.append(lax.ppermute(sent, "dp", pairs))
    by_row = jnp.stack(by_row)
    mine = jnp.stack(
        [jnp.take(by_row, (zl - prefix_owner[p] // 4) % 4, axis=0)[p] for p in range(2)]
    )
    mine, tied = lax.optimization_barrier((mine, tied))
    gathered = lax.all_gather(mine, "dp", axis=2, tiled=False)
    return gathered.reshape(gathered.shape[:2] + (-1,) + gathered.shape[4:]), tied


def _prefix_kernel(pick_ref, q_ref, kv_ref, m_ref, l_ref, acc_ref):
    q = q_ref[...]
    dims = (((1,), (1,)), ((), ()))
    first = pick_ref[...] == 0
    s0 = lax.dot_general(q, kv_ref[0, 0], dims, preferred_element_type=jnp.float32)
    s1 = lax.dot_general(q, kv_ref[1, 0], dims, preferred_element_type=jnp.float32)
    scores = jnp.where(first, s0, s1) * (HD ** (-0.5))
    top = jnp.max(scores, axis=1, keepdims=True)
    weights = jnp.exp(scores - top)
    m_ref[...] = top
    l_ref[...] = jnp.sum(weights, axis=1, keepdims=True)
    rounded = weights.astype(jnp.bfloat16)
    a0 = jnp.dot(rounded, kv_ref[0, 1], preferred_element_type=jnp.float32)
    a1 = jnp.dot(rounded, kv_ref[1, 1], preferred_element_type=jnp.float32)
    acc_ref[...] = jnp.where(first, a0, a1)


def prefix_attention(queries, both_prefixes, prefix_pick, block=128):
    rows, width = queries.shape
    kv_shape = both_prefixes.shape
    col = pl.BlockSpec((block, 1), lambda i: (i, 0))
    return pl.pallas_call(
        _prefix_kernel,
        grid=(rows // block,),
        in_specs=[
            col,
            pl.BlockSpec((block, width), lambda i: (i, 0)),
            pl.BlockSpec(kv_shape, lambda i: (0, 0, 0, 0)),
        ],
        out_specs=[col, col, pl.BlockSpec((block, width), lambda i: (i, 0))],
        out_shape=[
            jax.ShapeDtypeStruct((rows, 1), jnp.float32),
            jax.ShapeDtypeStruct((rows, 1), jnp.float32),
            jax.ShapeDtypeStruct((rows, width), jnp.float32),
        ],
    )(prefix_pick.reshape(rows, 1).astype(jnp.int32), queries, both_prefixes)


def slot_plan(lengths, prefix_id, placement_perm, group_index):
    requests = lax.dynamic_slice(placement_perm, (group_index * REQ_GRP,), (REQ_GRP,))
    req_sizes = jnp.take(lengths, requests)
    starts = jnp.cumsum(req_sizes) - req_sizes
    slot_ids = jnp.arange(CAP, dtype=jnp.int32)
    inside = (
        (slot_ids[None, :] >= starts[:, None]) & (slot_ids[None, :] < (starts + req_sizes)[:, None])
    ).astype(jnp.int32)
    live_slots = jnp.sum(inside, axis=0) > 0
    numbers = jnp.arange(1, REQ_GRP + 1, dtype=jnp.int32)
    owner_req = jnp.sum(inside * numbers[:, None], axis=0) - 1
    offsets = slot_ids - jnp.sum(inside * starts[:, None], axis=0)
    prefix_pick = jnp.sum(inside * jnp.take(prefix_id, requests)[:, None], axis=0)
    return (slot_ids, live_slots, owner_req, offsets, prefix_pick)


def rotate(values, offsets):
    half_dim = HD // 2
    inverse = jnp.power(ROPE_BASE, -2.0 * jnp.arange(half_dim, dtype=jnp.float32) / HD)
    angles = (offsets.astype(jnp.float32) + PLEN)[:, None] * inverse[None, :]
    cosine = jnp.cos(angles)[:, None, :]
    sine_part = jnp.sin(angles)[:, None, :]
    front_half = values[..., :half_dim]
    back_half = values[..., half_dim:]
    return jnp.concatenate(
        [front_half * cosine - back_half * sine_part, back_half * cosine + front_half * sine_part],
        axis=-1,
    )


def rms_scale(values, gain):
    mean_square = jnp.mean(values * values, axis=-1, keepdims=True)
    return values * lax.rsqrt(mean_square + EPSILON) * gain


def partial_softmax(scores, value_heads):
    running_max = jnp.max(scores, axis=-1, keepdims=True)
    weights = jnp.exp(scores - running_max)
    weight_sum = jnp.sum(weights, axis=-1, keepdims=True)
    accumulated = jnp.einsum(
        "hck,khd->hcd",
        weights.astype(jnp.bfloat16),
        value_heads,
        preferred_element_type=jnp.float32,
    )
    return (running_max, weight_sum, accumulated)


def merge_partials(partials):
    running_max = partials[0][0]
    for member in partials[1:]:
        running_max = jnp.maximum(running_max, member[0])
    weight_sum = jnp.zeros_like(partials[0][1])
    accumulated = jnp.zeros_like(partials[0][2])
    for member in partials:
        factor = jnp.exp(member[0] - running_max)
        weight_sum = weight_sum + factor * member[1]
        accumulated = accumulated + factor * member[2]
    return accumulated / weight_sum


def body(
    hidden,
    lengths,
    prefix_id,
    placement_perm,
    prefix_owner,
    prefix_cache,
    qkv_weight,
    q_gain,
    k_gain,
    out_weight,
    attn_gain,
    gate_up_weight,
    down_weight,
    mlp_gain,
):
    tensor_rank = lax.axis_index("tensor")
    group_index = lax.axis_index("dp")
    slot_ids, live_slots, owner_req, offsets, prefix_pick = slot_plan(
        lengths, prefix_id, placement_perm, group_index
    )
    local_rows = hidden.shape[0]
    local_width = qkv_weight.shape[2]
    local_heads = local_width // HD
    assert local_heads == 1
    row_start = tensor_rank * local_rows
    column_start = tensor_rank * local_width
    score_scale = HD ** (-0.5)
    both_prefixes, hidden = fetch_prefixes(prefix_cache[0], prefix_owner, hidden)
    full_rows = ag_tensor(hidden)
    projected = jnp.einsum("cd,kde->kce", full_rows, qkv_weight, preferred_element_type=jnp.float32)
    norm_gains = jnp.stack(
        [
            lax.dynamic_slice_in_dim(q_gain, column_start, local_width),
            lax.dynamic_slice_in_dim(k_gain, column_start, local_width),
        ]
    )
    squares = jnp.sum(projected[:2] * projected[:2], axis=2)
    totals = psum_tensor_f32(squares)
    normed = projected[:2] * lax.rsqrt(totals / D + EPSILON)[:, :, None] * norm_gains[:, None, :]
    queries = rotate(normed[0].reshape(CAP, local_heads, HD), offsets).astype(jnp.bfloat16)
    key_heads = rotate(normed[1].reshape(CAP, local_heads, HD), offsets).astype(jnp.bfloat16)
    value_heads = projected[2].astype(jnp.bfloat16).reshape(CAP, local_heads, HD)
    suf_scores = (
        jnp.einsum("chd,khd->hck", queries, key_heads, preferred_element_type=jnp.float32)
        * score_scale
    )
    visible = (
        (owner_req[:, None] == owner_req[None, :])
        & live_slots[None, :]
        & (slot_ids[None, :] <= slot_ids[:, None])
    )
    suf_scores = jnp.where(visible[None], suf_scores, MASKED_SCORE)
    partials = [partial_softmax(suf_scores, value_heads)]
    top, total, acc = prefix_attention(queries.reshape(CAP, HD), both_prefixes, prefix_pick)
    partials.append((top[None], total[None], acc[None]))
    attended = merge_partials(partials).astype(jnp.bfloat16)
    attended = attended.transpose(1, 0, 2).reshape(CAP, local_width)
    summed = rs_tensor(
        jnp.dot(attended, out_weight, preferred_element_type=jnp.float32).astype(jnp.bfloat16)
    )
    mid_rows = (hidden.astype(jnp.float32) + rms_scale(summed, attn_gain)).astype(jnp.bfloat16)
    merged = ag_tensor(mid_rows)
    gate_up = jnp.einsum("cd,kdf->kcf", merged, gate_up_weight, preferred_element_type=jnp.float32)
    activated = (jax.nn.silu(gate_up[0]) * gate_up[1]).astype(jnp.bfloat16)
    mlp_term = rs_tensor(
        jnp.dot(activated, down_weight, preferred_element_type=jnp.float32).astype(jnp.bfloat16)
    )
    result = mid_rows.astype(jnp.float32) + rms_scale(mlp_term, mlp_gain)
    live_rows = lax.dynamic_slice_in_dim(live_slots, row_start, local_rows, 0)
    hidden_out = jnp.where(live_rows[:, None], result, 0.0).astype(jnp.bfloat16)
    key_out = jnp.where(live_slots[:, None], key_heads.reshape(CAP, local_width), 0.0)
    value_out = jnp.where(live_slots[:, None], value_heads.reshape(CAP, local_width), 0.0)
    suffix_kv = jnp.stack([key_out, value_out])
    return (hidden_out, suffix_kv)


def solution(mesh):
    in_specs = (
        P(("dp", "tensor"), None),
        P(),
        P(),
        P(),
        P(),
        P("dp", None, None, "tensor"),
        P(None, None, "tensor"),
        P(),
        P(),
        P("tensor", None),
        P(),
        P(None, None, "tensor"),
        P("tensor", None),
        P(),
    )
    out_specs = (P(("dp", "tensor"), None), P(None, "dp", "tensor"))
    return jax.shard_map(body, mesh=mesh, in_specs=in_specs, out_specs=out_specs, check_vma=False)
```

```python
import jax
import jax.numpy as jnp
from jax import lax
from jax.sharding import PartitionSpec as P
from jax.experimental import pallas as pl
from jax.experimental.pallas import tpu as pltpu

D = 2048
HD = 128
CAP = 768
REQ_GRP = 4
PLEN = 4096


ROPE_BASE = 500000.0
EPSILON = 1e-06
MASKED_SCORE = -1e30


def from_root(shard, axis, root):
    mine = lax.axis_index(axis) == root
    return lax.psum(jnp.where(mine, shard, jnp.zeros_like(shard)), axis)


def _pairs(fn, n=16):
    return [(t, fn(t) % n) for t in range(n)]


def tensor_coords():
    t = lax.axis_index("tensor")
    return t // 4, (t // 2) % 2, t % 2


def ag_tensor_halves(block):
    x_i, zh, c = tensor_coords()
    other = lax.ppermute(block, "tensor", _pairs(lambda t: t ^ 2))
    pair = jnp.where(zh == 0, jnp.stack([block, other]), jnp.stack([other, block]))
    from_x = [lax.ppermute(pair, "tensor", _pairs(lambda t, k=k: t + 4 * k)) for k in (3, 2, 1)]
    quad = jnp.roll(jnp.stack([pair] + from_x), x_i, axis=0)
    mate = lax.ppermute(quad, "tensor", _pairs(lambda t: t ^ 1))
    return quad, mate


def ag_tensor(block):
    x_i, zh, c = tensor_coords()
    quad, mate = ag_tensor_halves(block)
    full = jnp.where(c == 0, jnp.stack([quad, mate], axis=2), jnp.stack([mate, quad], axis=2))
    return full.reshape((-1,) + block.shape[1:])


def rs_tensor(rows):
    x_i, zh, c = tensor_coords()
    grid = rows.reshape((4, 2, 2, -1) + rows.shape[1:])
    mine = jnp.take(grid, c, axis=2)
    theirs = jnp.take(grid, 1 - c, axis=2)
    return rs_tensor_halves(mine, theirs)


def rs_tensor_halves(mine, theirs):
    x_i, zh, c = tensor_coords()
    sent = theirs.astype(jnp.bfloat16)
    got = lax.ppermute(sent, "tensor", _pairs(lambda t: t ^ 1))
    summed = mine.astype(jnp.float32) + got.astype(jnp.float32)
    rel = jnp.roll(summed, -x_i, axis=0)
    total = rel[0]
    for k in (1, 2, 3):
        sent = rel[k].astype(jnp.bfloat16)
        total = total + lax.ppermute(sent, "tensor", _pairs(lambda t, k=k: t + 4 * k)).astype(jnp.float32)
    mine = jnp.take(total, zh, axis=0)
    theirs = jnp.take(total, 1 - zh, axis=0).astype(jnp.bfloat16)
    return mine + lax.ppermute(theirs, "tensor", _pairs(lambda t: t ^ 2)).astype(jnp.float32)


def psum_tensor_f32(values):
    values = values + lax.ppermute(values, "tensor", _pairs(lambda t: t ^ 1))
    values = values + lax.ppermute(values, "tensor", _pairs(lambda t: t ^ 2))
    shifted = [lax.ppermute(values, "tensor", _pairs(lambda t, k=k: t + 4 * k)) for k in (1, 2, 3)]
    return values + shifted[0] + shifted[1] + shifted[2]


def fetch_prefixes(own_slot, prefix_owner, tied):
    g = lax.axis_index("dp")
    zl, y = g // 4, g % 4
    cols = own_slot.reshape((own_slot.shape[0], 4, 4, -1) + own_slot.shape[2:])
    by_col = [jnp.take(cols, y, axis=2)]
    for k in (1, 2, 3):
        sent = jnp.take(cols, (y + k) % 4, axis=2)
        pairs = _pairs(lambda i, k=k: (i // 4) * 4 + (i % 4 + k) % 4)
        by_col.append(lax.ppermute(sent, "dp", pairs))
    by_col = jnp.stack(by_col)
    rows = jnp.stack([jnp.take(by_col, (y - prefix_owner[p] % 4) % 4, axis=0) for p in range(2)])
    by_row = [jnp.take(rows, zl, axis=2)]
    for k in (1, 2, 3):
        sent = jnp.take(rows, (zl + k) % 4, axis=2)
        pairs = _pairs(lambda i, k=k: ((i // 4 + k) % 4) * 4 + i % 4)
        by_row.append(lax.ppermute(sent, "dp", pairs))
    by_row = jnp.stack(by_row)
    mine = jnp.stack(
        [jnp.take(by_row, (zl - prefix_owner[p] // 4) % 4, axis=0)[p] for p in range(2)]
    )
    mine, tied = lax.optimization_barrier((mine, tied))
    gathered = lax.all_gather(mine, "dp", axis=2, tiled=False)
    return gathered.reshape(gathered.shape[:2] + (-1,) + gathered.shape[4:]), tied


def _prefix_kernel(pick_ref, q_ref, kv_ref, m_ref, l_ref, acc_ref):
    q = q_ref[...]
    dims = (((1,), (1,)), ((), ()))
    first = pick_ref[...] == 0
    s0 = lax.dot_general(q, kv_ref[0, 0], dims, preferred_element_type=jnp.float32)
    s1 = lax.dot_general(q, kv_ref[1, 0], dims, preferred_element_type=jnp.float32)
    scores = jnp.where(first, s0, s1) * (HD ** (-0.5))
    top = jnp.max(scores, axis=1, keepdims=True)
    weights = jnp.exp(scores - top)
    m_ref[...] = top
    l_ref[...] = jnp.sum(weights, axis=1, keepdims=True)
    rounded = weights.astype(jnp.bfloat16)
    a0 = jnp.dot(rounded, kv_ref[0, 1], preferred_element_type=jnp.float32)
    a1 = jnp.dot(rounded, kv_ref[1, 1], preferred_element_type=jnp.float32)
    acc_ref[...] = jnp.where(first, a0, a1)


def prefix_attention(queries, both_prefixes, prefix_pick, block=128):
    rows, width = queries.shape
    kv_shape = both_prefixes.shape
    col = pl.BlockSpec((block, 1), lambda i: (i, 0))
    return pl.pallas_call(
        _prefix_kernel,
        grid=(rows // block,),
        in_specs=[
            col,
            pl.BlockSpec((block, width), lambda i: (i, 0)),
            pl.BlockSpec(kv_shape, lambda i: (0, 0, 0, 0)),
        ],
        out_specs=[col, col, pl.BlockSpec((block, width), lambda i: (i, 0))],
        out_shape=[
            jax.ShapeDtypeStruct((rows, 1), jnp.float32),
            jax.ShapeDtypeStruct((rows, 1), jnp.float32),
            jax.ShapeDtypeStruct((rows, width), jnp.float32),
        ],
    )(prefix_pick.reshape(rows, 1).astype(jnp.int32), queries, both_prefixes)


def slot_plan(lengths, prefix_id, placement_perm, group_index):
    requests = lax.dynamic_slice(placement_perm, (group_index * REQ_GRP,), (REQ_GRP,))
    req_sizes = jnp.take(lengths, requests)
    starts = jnp.cumsum(req_sizes) - req_sizes
    slot_ids = jnp.arange(CAP, dtype=jnp.int32)
    inside = (
        (slot_ids[None, :] >= starts[:, None]) & (slot_ids[None, :] < (starts + req_sizes)[:, None])
    ).astype(jnp.int32)
    live_slots = jnp.sum(inside, axis=0) > 0
    numbers = jnp.arange(1, REQ_GRP + 1, dtype=jnp.int32)
    owner_req = jnp.sum(inside * numbers[:, None], axis=0) - 1
    offsets = slot_ids - jnp.sum(inside * starts[:, None], axis=0)
    prefix_pick = jnp.sum(inside * jnp.take(prefix_id, requests)[:, None], axis=0)
    return (slot_ids, live_slots, owner_req, offsets, prefix_pick)


def rotate(values, offsets):
    half_dim = HD // 2
    inverse = jnp.power(ROPE_BASE, -2.0 * jnp.arange(half_dim, dtype=jnp.float32) / HD)
    angles = (offsets.astype(jnp.float32) + PLEN)[:, None] * inverse[None, :]
    cosine = jnp.cos(angles)[:, None, :]
    sine_part = jnp.sin(angles)[:, None, :]
    front_half = values[..., :half_dim]
    back_half = values[..., half_dim:]
    return jnp.concatenate(
        [front_half * cosine - back_half * sine_part, back_half * cosine + front_half * sine_part],
        axis=-1,
    )


def rms_scale(values, gain):
    mean_square = jnp.mean(values * values, axis=-1, keepdims=True)
    return values * lax.rsqrt(mean_square + EPSILON) * gain


def partial_softmax(scores, value_heads):
    running_max = jnp.max(scores, axis=-1, keepdims=True)
    weights = jnp.exp(scores - running_max)
    weight_sum = jnp.sum(weights, axis=-1, keepdims=True)
    accumulated = jnp.einsum(
        "hck,khd->hcd",
        weights.astype(jnp.bfloat16),
        value_heads,
        preferred_element_type=jnp.float32,
    )
    return (running_max, weight_sum, accumulated)


def merge_partials(partials):
    running_max = partials[0][0]
    for member in partials[1:]:
        running_max = jnp.maximum(running_max, member[0])
    weight_sum = jnp.zeros_like(partials[0][1])
    accumulated = jnp.zeros_like(partials[0][2])
    for member in partials:
        factor = jnp.exp(member[0] - running_max)
        weight_sum = weight_sum + factor * member[1]
        accumulated = accumulated + factor * member[2]
    return accumulated / weight_sum


def body(
    hidden,
    lengths,
    prefix_id,
    placement_perm,
    prefix_owner,
    prefix_cache,
    qkv_weight,
    q_gain,
    k_gain,
    out_weight,
    attn_gain,
    gate_up_weight,
    down_weight,
    mlp_gain,
):
    tensor_rank = lax.axis_index("tensor")
    group_index = lax.axis_index("dp")
    slot_ids, live_slots, owner_req, offsets, prefix_pick = slot_plan(
        lengths, prefix_id, placement_perm, group_index
    )
    local_rows = hidden.shape[0]
    local_width = qkv_weight.shape[2]
    local_heads = local_width // HD
    assert local_heads == 1
    row_start = tensor_rank * local_rows
    column_start = tensor_rank * local_width
    score_scale = HD ** (-0.5)
    both_prefixes, hidden = fetch_prefixes(prefix_cache[0], prefix_owner, hidden)
    full_rows = ag_tensor(hidden)
    projected = jnp.einsum("cd,kde->kce", full_rows, qkv_weight, preferred_element_type=jnp.float32)
    norm_gains = jnp.stack(
        [
            lax.dynamic_slice_in_dim(q_gain, column_start, local_width),
            lax.dynamic_slice_in_dim(k_gain, column_start, local_width),
        ]
    )
    squares = jnp.sum(projected[:2] * projected[:2], axis=2)
    totals = psum_tensor_f32(squares)
    normed = projected[:2] * lax.rsqrt(totals / D + EPSILON)[:, :, None] * norm_gains[:, None, :]
    queries = rotate(normed[0].reshape(CAP, local_heads, HD), offsets).astype(jnp.bfloat16)
    key_heads = rotate(normed[1].reshape(CAP, local_heads, HD), offsets).astype(jnp.bfloat16)
    value_heads = projected[2].astype(jnp.bfloat16).reshape(CAP, local_heads, HD)
    suf_scores = (
        jnp.einsum("chd,khd->hck", queries, key_heads, preferred_element_type=jnp.float32)
        * score_scale
    )
    visible = (
        (owner_req[:, None] == owner_req[None, :])
        & live_slots[None, :]
        & (slot_ids[None, :] <= slot_ids[:, None])
    )
    suf_scores = jnp.where(visible[None], suf_scores, MASKED_SCORE)
    partials = [partial_softmax(suf_scores, value_heads)]
    top, total, acc = prefix_attention(queries.reshape(CAP, HD), both_prefixes, prefix_pick)
    partials.append((top[None], total[None], acc[None]))
    attended = merge_partials(partials).astype(jnp.bfloat16)
    attended = attended.transpose(1, 0, 2).reshape(CAP, local_width)
    summed = rs_tensor(
        jnp.dot(attended, out_weight, preferred_element_type=jnp.float32).astype(jnp.bfloat16)
    )
    mid_rows = (hidden.astype(jnp.float32) + rms_scale(summed, attn_gain)).astype(jnp.bfloat16)
    quad, mate = ag_tensor_halves(mid_rows)

    def mlp_part(rows):
        flat = rows.reshape(-1, rows.shape[-1])
        gate_up = jnp.einsum("cd,kdf->kcf", flat, gate_up_weight, preferred_element_type=jnp.float32)
        activated = (jax.nn.silu(gate_up[0]) * gate_up[1]).astype(jnp.bfloat16)
        down = jnp.dot(activated, down_weight, preferred_element_type=jnp.float32)
        return down.astype(jnp.bfloat16).reshape(rows.shape)

    mlp_term = rs_tensor_halves(mlp_part(quad), mlp_part(mate))
    result = mid_rows.astype(jnp.float32) + rms_scale(mlp_term, mlp_gain)
    live_rows = lax.dynamic_slice_in_dim(live_slots, row_start, local_rows, 0)
    hidden_out = jnp.where(live_rows[:, None], result, 0.0).astype(jnp.bfloat16)
    key_out = jnp.where(live_slots[:, None], key_heads.reshape(CAP, local_width), 0.0)
    value_out = jnp.where(live_slots[:, None], value_heads.reshape(CAP, local_width), 0.0)
    suffix_kv = jnp.stack([key_out, value_out])
    return (hidden_out, suffix_kv)


def solution(mesh):
    in_specs = (
        P(("dp", "tensor"), None),
        P(),
        P(),
        P(),
        P(),
        P("dp", None, None, "tensor"),
        P(None, None, "tensor"),
        P(),
        P(),
        P("tensor", None),
        P(),
        P(None, None, "tensor"),
        P("tensor", None),
        P(),
    )
    out_specs = (P(("dp", "tensor"), None), P(None, "dp", "tensor"))
    return jax.shard_map(body, mesh=mesh, in_specs=in_specs, out_specs=out_specs, check_vma=False)
```

```python
import jax
import jax.numpy as jnp
from jax import lax
from jax.sharding import PartitionSpec as P
from jax.experimental import pallas as pl
from jax.experimental.pallas import tpu as pltpu

D = 2048
HD = 128
CAP = 768
REQ_GRP = 4
PLEN = 4096


ROPE_BASE = 500000.0
EPSILON = 1e-06
MASKED_SCORE = -1e30


def from_root(shard, axis, root):
    mine = lax.axis_index(axis) == root
    return lax.psum(jnp.where(mine, shard, jnp.zeros_like(shard)), axis)


def _pairs(fn, n=16):
    return [(t, fn(t) % n) for t in range(n)]


def tensor_coords():
    t = lax.axis_index("tensor")
    return t // 4, (t // 2) % 2, t % 2


def ag_tensor_halves(block):
    x_i, zh, c = tensor_coords()
    other = lax.ppermute(block, "tensor", _pairs(lambda t: t ^ 2))
    pair = jnp.where(zh == 0, jnp.stack([block, other]), jnp.stack([other, block]))
    from_x = [lax.ppermute(pair, "tensor", _pairs(lambda t, k=k: t + 4 * k)) for k in (3, 2, 1)]
    quad = jnp.roll(jnp.stack([pair] + from_x), x_i, axis=0)
    mate = lax.ppermute(quad, "tensor", _pairs(lambda t: t ^ 1))
    return quad, mate


def ag_tensor(block):
    x_i, zh, c = tensor_coords()
    quad, mate = ag_tensor_halves(block)
    full = jnp.where(c == 0, jnp.stack([quad, mate], axis=2), jnp.stack([mate, quad], axis=2))
    return full.reshape((-1,) + block.shape[1:])


def rs_tensor(rows):
    x_i, zh, c = tensor_coords()
    grid = rows.reshape((4, 2, 2, -1) + rows.shape[1:])
    mine = jnp.take(grid, c, axis=2)
    theirs = jnp.take(grid, 1 - c, axis=2)
    return rs_tensor_halves(mine, theirs)


def rs_tensor_halves(mine, theirs):
    x_i, zh, c = tensor_coords()
    sent = theirs.astype(jnp.bfloat16)
    got = lax.ppermute(sent, "tensor", _pairs(lambda t: t ^ 1))
    summed = mine.astype(jnp.float32) + got.astype(jnp.float32)
    rel = jnp.roll(summed, -x_i, axis=0)
    total = rel[0]
    for k in (1, 2, 3):
        sent = rel[k].astype(jnp.bfloat16)
        total = total + lax.ppermute(sent, "tensor", _pairs(lambda t, k=k: t + 4 * k)).astype(jnp.float32)
    mine = jnp.take(total, zh, axis=0)
    theirs = jnp.take(total, 1 - zh, axis=0).astype(jnp.bfloat16)
    return mine + lax.ppermute(theirs, "tensor", _pairs(lambda t: t ^ 2)).astype(jnp.float32)


def psum_tensor_f32(values):
    values = values + lax.ppermute(values, "tensor", _pairs(lambda t: t ^ 1))
    values = values + lax.ppermute(values, "tensor", _pairs(lambda t: t ^ 2))
    shifted = [lax.ppermute(values, "tensor", _pairs(lambda t, k=k: t + 4 * k)) for k in (1, 2, 3)]
    return values + shifted[0] + shifted[1] + shifted[2]


def fetch_prefixes(own_slot, prefix_owner, tied):
    g = lax.axis_index("dp")
    zl, y = g // 4, g % 4
    cols = own_slot.reshape((own_slot.shape[0], 4, 4, -1) + own_slot.shape[2:])
    by_col = [jnp.take(cols, y, axis=2)]
    for k in (1, 2, 3):
        sent = jnp.take(cols, (y + k) % 4, axis=2)
        pairs = _pairs(lambda i, k=k: (i // 4) * 4 + (i % 4 + k) % 4)
        by_col.append(lax.ppermute(sent, "dp", pairs))
    by_col = jnp.stack(by_col)
    rows = jnp.stack([jnp.take(by_col, (y - prefix_owner[p] % 4) % 4, axis=0) for p in range(2)])
    by_row = [jnp.take(rows, zl, axis=2)]
    for k in (1, 2, 3):
        sent = jnp.take(rows, (zl + k) % 4, axis=2)
        pairs = _pairs(lambda i, k=k: ((i // 4 + k) % 4) * 4 + i % 4)
        by_row.append(lax.ppermute(sent, "dp", pairs))
    by_row = jnp.stack(by_row)
    mine = jnp.stack(
        [jnp.take(by_row, (zl - prefix_owner[p] // 4) % 4, axis=0)[p] for p in range(2)]
    )
    mine, tied = lax.optimization_barrier((mine, tied))
    gathered = lax.all_gather(mine, "dp", axis=2, tiled=False)
    return gathered.reshape(gathered.shape[:2] + (-1,) + gathered.shape[4:]), tied


def _prefix_kernel(pick_ref, q_ref, kv_ref, m_ref, l_ref, acc_ref):
    q = q_ref[...]
    dims = (((1,), (1,)), ((), ()))
    first = pick_ref[...] == 0
    s0 = lax.dot_general(q, kv_ref[0, 0], dims, preferred_element_type=jnp.float32)
    s1 = lax.dot_general(q, kv_ref[1, 0], dims, preferred_element_type=jnp.float32)
    scores = jnp.where(first, s0, s1) * (HD ** (-0.5))
    top = jnp.max(scores, axis=1, keepdims=True)
    weights = jnp.exp(scores - top)
    m_ref[...] = top
    l_ref[...] = jnp.sum(weights, axis=1, keepdims=True)
    rounded = weights.astype(jnp.bfloat16)
    a0 = jnp.dot(rounded, kv_ref[0, 1], preferred_element_type=jnp.float32)
    a1 = jnp.dot(rounded, kv_ref[1, 1], preferred_element_type=jnp.float32)
    acc_ref[...] = jnp.where(first, a0, a1)


def prefix_attention(queries, both_prefixes, prefix_pick, block=128):
    rows, width = queries.shape
    kv_shape = both_prefixes.shape
    col = pl.BlockSpec((block, 1), lambda i: (i, 0))
    return pl.pallas_call(
        _prefix_kernel,
        grid=(rows // block,),
        in_specs=[
            col,
            pl.BlockSpec((block, width), lambda i: (i, 0)),
            pl.BlockSpec(kv_shape, lambda i: (0, 0, 0, 0)),
        ],
        out_specs=[col, col, pl.BlockSpec((block, width), lambda i: (i, 0))],
        out_shape=[
            jax.ShapeDtypeStruct((rows, 1), jnp.float32),
            jax.ShapeDtypeStruct((rows, 1), jnp.float32),
            jax.ShapeDtypeStruct((rows, width), jnp.float32),
        ],
    )(prefix_pick.reshape(rows, 1).astype(jnp.int32), queries, both_prefixes)


def slot_plan(lengths, prefix_id, placement_perm, group_index):
    requests = lax.dynamic_slice(placement_perm, (group_index * REQ_GRP,), (REQ_GRP,))
    req_sizes = jnp.take(lengths, requests)
    starts = jnp.cumsum(req_sizes) - req_sizes
    slot_ids = jnp.arange(CAP, dtype=jnp.int32)
    inside = (
        (slot_ids[None, :] >= starts[:, None]) & (slot_ids[None, :] < (starts + req_sizes)[:, None])
    ).astype(jnp.int32)
    live_slots = jnp.sum(inside, axis=0) > 0
    numbers = jnp.arange(1, REQ_GRP + 1, dtype=jnp.int32)
    owner_req = jnp.sum(inside * numbers[:, None], axis=0) - 1
    offsets = slot_ids - jnp.sum(inside * starts[:, None], axis=0)
    prefix_pick = jnp.sum(inside * jnp.take(prefix_id, requests)[:, None], axis=0)
    return (slot_ids, live_slots, owner_req, offsets, prefix_pick)


def rotate(values, offsets):
    half_dim = HD // 2
    inverse = jnp.power(ROPE_BASE, -2.0 * jnp.arange(half_dim, dtype=jnp.float32) / HD)
    angles = (offsets.astype(jnp.float32) + PLEN)[:, None] * inverse[None, :]
    cosine = jnp.cos(angles)[:, None, :]
    sine_part = jnp.sin(angles)[:, None, :]
    front_half = values[..., :half_dim]
    back_half = values[..., half_dim:]
    return jnp.concatenate(
        [front_half * cosine - back_half * sine_part, back_half * cosine + front_half * sine_part],
        axis=-1,
    )


def rms_scale(values, gain):
    mean_square = jnp.mean(values * values, axis=-1, keepdims=True)
    return values * lax.rsqrt(mean_square + EPSILON) * gain


def partial_softmax(scores, value_heads):
    running_max = jnp.max(scores, axis=-1, keepdims=True)
    weights = jnp.exp(scores - running_max)
    weight_sum = jnp.sum(weights, axis=-1, keepdims=True)
    accumulated = jnp.einsum(
        "hck,khd->hcd",
        weights.astype(jnp.bfloat16),
        value_heads,
        preferred_element_type=jnp.float32,
    )
    return (running_max, weight_sum, accumulated)


def merge_partials(partials):
    running_max = partials[0][0]
    for member in partials[1:]:
        running_max = jnp.maximum(running_max, member[0])
    weight_sum = jnp.zeros_like(partials[0][1])
    accumulated = jnp.zeros_like(partials[0][2])
    for member in partials:
        factor = jnp.exp(member[0] - running_max)
        weight_sum = weight_sum + factor * member[1]
        accumulated = accumulated + factor * member[2]
    return accumulated / weight_sum


def body(
    hidden,
    lengths,
    prefix_id,
    placement_perm,
    prefix_owner,
    prefix_cache,
    qkv_weight,
    q_gain,
    k_gain,
    out_weight,
    attn_gain,
    gate_up_weight,
    down_weight,
    mlp_gain,
):
    tensor_rank = lax.axis_index("tensor")
    group_index = lax.axis_index("dp")
    slot_ids, live_slots, owner_req, offsets, prefix_pick = slot_plan(
        lengths, prefix_id, placement_perm, group_index
    )
    local_rows = hidden.shape[0]
    local_width = qkv_weight.shape[2]
    local_heads = local_width // HD
    assert local_heads == 1
    row_start = tensor_rank * local_rows
    column_start = tensor_rank * local_width
    score_scale = HD ** (-0.5)
    both_prefixes, hidden = fetch_prefixes(prefix_cache[0], prefix_owner, hidden)
    full_rows = ag_tensor(hidden)
    projected = jnp.einsum("cd,kde->kce", full_rows, qkv_weight, preferred_element_type=jnp.float32)
    norm_gains = jnp.stack(
        [
            lax.dynamic_slice_in_dim(q_gain, column_start, local_width),
            lax.dynamic_slice_in_dim(k_gain, column_start, local_width),
        ]
    )
    squares = jnp.sum(projected[:2] * projected[:2], axis=2)
    totals = psum_tensor_f32(squares)
    normed = projected[:2] * lax.rsqrt(totals / D + EPSILON)[:, :, None] * norm_gains[:, None, :]
    queries = rotate(normed[0].reshape(CAP, local_heads, HD), offsets).astype(jnp.bfloat16)
    key_heads = rotate(normed[1].reshape(CAP, local_heads, HD), offsets).astype(jnp.bfloat16)
    value_heads = projected[2].astype(jnp.bfloat16).reshape(CAP, local_heads, HD)
    suf_scores = (
        jnp.einsum("chd,khd->hck", queries, key_heads, preferred_element_type=jnp.float32)
        * score_scale
    )
    visible = (
        (owner_req[:, None] == owner_req[None, :])
        & live_slots[None, :]
        & (slot_ids[None, :] <= slot_ids[:, None])
    )
    suf_scores = jnp.where(visible[None], suf_scores, MASKED_SCORE)
    partials = [partial_softmax(suf_scores, value_heads)]
    top, total, acc = prefix_attention(queries.reshape(CAP, HD), both_prefixes, prefix_pick)
    partials.append((top[None], total[None], acc[None]))
    attended = merge_partials(partials).astype(jnp.bfloat16)
    attended = attended.transpose(1, 0, 2).reshape(CAP, local_width)
    by_core = attended.reshape((4, 2, 2, -1) + attended.shape[1:])
    my_core = tensor_coords()[2]

    def project(rows):
        flat = jnp.dot(rows.reshape(-1, rows.shape[-1]), out_weight, preferred_element_type=jnp.float32)
        return flat.astype(jnp.bfloat16).reshape(rows.shape[:-1] + (out_weight.shape[1],))

    summed = rs_tensor_halves(
        project(jnp.take(by_core, my_core, axis=2)), project(jnp.take(by_core, 1 - my_core, axis=2))
    )
    mid_rows = (hidden.astype(jnp.float32) + rms_scale(summed, attn_gain)).astype(jnp.bfloat16)
    quad, mate = ag_tensor_halves(mid_rows)

    def mlp_part(rows):
        flat = rows.reshape(-1, rows.shape[-1])
        gate_up = jnp.einsum("cd,kdf->kcf", flat, gate_up_weight, preferred_element_type=jnp.float32)
        activated = (jax.nn.silu(gate_up[0]) * gate_up[1]).astype(jnp.bfloat16)
        down = jnp.dot(activated, down_weight, preferred_element_type=jnp.float32)
        return down.astype(jnp.bfloat16).reshape(rows.shape)

    mlp_term = rs_tensor_halves(mlp_part(quad), mlp_part(mate))
    result = mid_rows.astype(jnp.float32) + rms_scale(mlp_term, mlp_gain)
    live_rows = lax.dynamic_slice_in_dim(live_slots, row_start, local_rows, 0)
    hidden_out = jnp.where(live_rows[:, None], result, 0.0).astype(jnp.bfloat16)
    key_out = jnp.where(live_slots[:, None], key_heads.reshape(CAP, local_width), 0.0)
    value_out = jnp.where(live_slots[:, None], value_heads.reshape(CAP, local_width), 0.0)
    suffix_kv = jnp.stack([key_out, value_out])
    return (hidden_out, suffix_kv)


def solution(mesh):
    in_specs = (
        P(("dp", "tensor"), None),
        P(),
        P(),
        P(),
        P(),
        P("dp", None, None, "tensor"),
        P(None, None, "tensor"),
        P(),
        P(),
        P("tensor", None),
        P(),
        P(None, None, "tensor"),
        P("tensor", None),
        P(),
    )
    out_specs = (P(("dp", "tensor"), None), P(None, "dp", "tensor"))
    return jax.shard_map(body, mesh=mesh, in_specs=in_specs, out_specs=out_specs, check_vma=False)
```

```python
import jax
import jax.numpy as jnp
from jax import lax
from jax.sharding import PartitionSpec as P
from jax.experimental import pallas as pl
from jax.experimental.pallas import tpu as pltpu

D = 2048
HD = 128
CAP = 768
REQ_GRP = 4
PLEN = 4096


ROPE_BASE = 500000.0
EPSILON = 1e-06
MASKED_SCORE = -1e30


def from_root(shard, axis, root):
    mine = lax.axis_index(axis) == root
    return lax.psum(jnp.where(mine, shard, jnp.zeros_like(shard)), axis)


def _pairs(fn, n=16):
    return [(t, fn(t) % n) for t in range(n)]


def tensor_coords():
    t = lax.axis_index("tensor")
    return t // 4, (t // 2) % 2, t % 2


def ag_tensor_halves(block):
    x_i, zh, c = tensor_coords()
    other = lax.ppermute(block, "tensor", _pairs(lambda t: t ^ 2))
    pair = jnp.where(zh == 0, jnp.stack([block, other]), jnp.stack([other, block]))
    from_x = [lax.ppermute(pair, "tensor", _pairs(lambda t, k=k: t + 4 * k)) for k in (3, 2, 1)]
    quad = jnp.roll(jnp.stack([pair] + from_x), x_i, axis=0)
    mate = lax.ppermute(quad, "tensor", _pairs(lambda t: t ^ 1))
    return quad, mate


def ag_tensor(block):
    x_i, zh, c = tensor_coords()
    quad, mate = ag_tensor_halves(block)
    full = jnp.where(c == 0, jnp.stack([quad, mate], axis=2), jnp.stack([mate, quad], axis=2))
    return full.reshape((-1,) + block.shape[1:])


def rs_tensor(rows):
    x_i, zh, c = tensor_coords()
    grid = rows.reshape((4, 2, 2, -1) + rows.shape[1:])
    mine = jnp.take(grid, c, axis=2)
    theirs = jnp.take(grid, 1 - c, axis=2)
    return rs_tensor_halves(mine, theirs)


def rs_tensor_halves(mine, theirs):
    x_i, zh, c = tensor_coords()
    sent = theirs.astype(jnp.bfloat16)
    got = lax.ppermute(sent, "tensor", _pairs(lambda t: t ^ 1))
    summed = mine.astype(jnp.float32) + got.astype(jnp.float32)
    rel = jnp.roll(summed, -x_i, axis=0)
    total = rel[0]
    for k in (1, 2, 3):
        sent = rel[k].astype(jnp.bfloat16)
        total = total + lax.ppermute(sent, "tensor", _pairs(lambda t, k=k: t + 4 * k)).astype(jnp.float32)
    mine = jnp.take(total, zh, axis=0)
    theirs = jnp.take(total, 1 - zh, axis=0).astype(jnp.bfloat16)
    return mine + lax.ppermute(theirs, "tensor", _pairs(lambda t: t ^ 2)).astype(jnp.float32)


def psum_tensor_f32(values):
    values = values + lax.ppermute(values, "tensor", _pairs(lambda t: t ^ 1))
    values = values + lax.ppermute(values, "tensor", _pairs(lambda t: t ^ 2))
    shifted = [lax.ppermute(values, "tensor", _pairs(lambda t, k=k: t + 4 * k)) for k in (1, 2, 3)]
    return values + shifted[0] + shifted[1] + shifted[2]


def fetch_prefixes(own_slot, prefix_owner, tied):
    g = lax.axis_index("dp")
    zl, y = g // 4, g % 4
    cols = own_slot.reshape((own_slot.shape[0], 4, 4, -1) + own_slot.shape[2:])
    by_col = [jnp.take(cols, y, axis=2)]
    for k in (1, 2, 3):
        sent = jnp.take(cols, (y + k) % 4, axis=2)
        pairs = _pairs(lambda i, k=k: (i // 4) * 4 + (i % 4 + k) % 4)
        by_col.append(lax.ppermute(sent, "dp", pairs))
    by_col = jnp.stack(by_col)
    rows = jnp.stack([jnp.take(by_col, (y - prefix_owner[p] % 4) % 4, axis=0) for p in range(2)])
    by_row = [jnp.take(rows, zl, axis=2)]
    for k in (1, 2, 3):
        sent = jnp.take(rows, (zl + k) % 4, axis=2)
        pairs = _pairs(lambda i, k=k: ((i // 4 + k) % 4) * 4 + i % 4)
        by_row.append(lax.ppermute(sent, "dp", pairs))
    by_row = jnp.stack(by_row)
    mine = jnp.stack(
        [jnp.take(by_row, (zl - prefix_owner[p] // 4) % 4, axis=0)[p] for p in range(2)]
    )
    mine, tied = lax.optimization_barrier((mine, tied))
    gathered = lax.all_gather(mine, "dp", axis=2, tiled=False)
    return gathered.reshape(gathered.shape[:2] + (-1,) + gathered.shape[4:]), tied


def _prefix_kernel(pick_ref, q_ref, kv_ref, m_ref, l_ref, acc_ref):
    q = q_ref[...]
    dims = (((1,), (1,)), ((), ()))
    first = pick_ref[...] == 0
    s0 = lax.dot_general(q, kv_ref[0, 0], dims, preferred_element_type=jnp.float32)
    s1 = lax.dot_general(q, kv_ref[1, 0], dims, preferred_element_type=jnp.float32)
    scores = jnp.where(first, s0, s1) * (HD ** (-0.5))
    top = jnp.max(scores, axis=1, keepdims=True)
    weights = jnp.exp(scores - top)
    m_ref[...] = top
    l_ref[...] = jnp.sum(weights, axis=1, keepdims=True)
    rounded = weights.astype(jnp.bfloat16)
    a0 = jnp.dot(rounded, kv_ref[0, 1], preferred_element_type=jnp.float32)
    a1 = jnp.dot(rounded, kv_ref[1, 1], preferred_element_type=jnp.float32)
    acc_ref[...] = jnp.where(first, a0, a1)


def prefix_attention(queries, both_prefixes, prefix_pick, block=256):
    rows, width = queries.shape
    kv_shape = both_prefixes.shape
    col = pl.BlockSpec((block, 1), lambda i: (i, 0))
    return pl.pallas_call(
        _prefix_kernel,
        grid=(rows // block,),
        in_specs=[
            col,
            pl.BlockSpec((block, width), lambda i: (i, 0)),
            pl.BlockSpec(kv_shape, lambda i: (0, 0, 0, 0)),
        ],
        out_specs=[col, col, pl.BlockSpec((block, width), lambda i: (i, 0))],
        out_shape=[
            jax.ShapeDtypeStruct((rows, 1), jnp.float32),
            jax.ShapeDtypeStruct((rows, 1), jnp.float32),
            jax.ShapeDtypeStruct((rows, width), jnp.float32),
        ],
    )(prefix_pick.reshape(rows, 1).astype(jnp.int32), queries, both_prefixes)


def slot_plan(lengths, prefix_id, placement_perm, group_index):
    requests = lax.dynamic_slice(placement_perm, (group_index * REQ_GRP,), (REQ_GRP,))
    req_sizes = jnp.take(lengths, requests)
    starts = jnp.cumsum(req_sizes) - req_sizes
    slot_ids = jnp.arange(CAP, dtype=jnp.int32)
    inside = (
        (slot_ids[None, :] >= starts[:, None]) & (slot_ids[None, :] < (starts + req_sizes)[:, None])
    ).astype(jnp.int32)
    live_slots = jnp.sum(inside, axis=0) > 0
    numbers = jnp.arange(1, REQ_GRP + 1, dtype=jnp.int32)
    owner_req = jnp.sum(inside * numbers[:, None], axis=0) - 1
    offsets = slot_ids - jnp.sum(inside * starts[:, None], axis=0)
    prefix_pick = jnp.sum(inside * jnp.take(prefix_id, requests)[:, None], axis=0)
    return (slot_ids, live_slots, owner_req, offsets, prefix_pick)


def rotate(values, offsets):
    half_dim = HD // 2
    inverse = jnp.power(ROPE_BASE, -2.0 * jnp.arange(half_dim, dtype=jnp.float32) / HD)
    angles = (offsets.astype(jnp.float32) + PLEN)[:, None] * inverse[None, :]
    cosine = jnp.cos(angles)[:, None, :]
    sine_part = jnp.sin(angles)[:, None, :]
    front_half = values[..., :half_dim]
    back_half = values[..., half_dim:]
    return jnp.concatenate(
        [front_half * cosine - back_half * sine_part, back_half * cosine + front_half * sine_part],
        axis=-1,
    )


def rms_scale(values, gain):
    mean_square = jnp.mean(values * values, axis=-1, keepdims=True)
    return values * lax.rsqrt(mean_square + EPSILON) * gain


def partial_softmax(scores, value_heads):
    running_max = jnp.max(scores, axis=-1, keepdims=True)
    weights = jnp.exp(scores - running_max)
    weight_sum = jnp.sum(weights, axis=-1, keepdims=True)
    accumulated = jnp.einsum(
        "hck,khd->hcd",
        weights.astype(jnp.bfloat16),
        value_heads,
        preferred_element_type=jnp.float32,
    )
    return (running_max, weight_sum, accumulated)


def merge_partials(partials):
    running_max = partials[0][0]
    for member in partials[1:]:
        running_max = jnp.maximum(running_max, member[0])
    weight_sum = jnp.zeros_like(partials[0][1])
    accumulated = jnp.zeros_like(partials[0][2])
    for member in partials:
        factor = jnp.exp(member[0] - running_max)
        weight_sum = weight_sum + factor * member[1]
        accumulated = accumulated + factor * member[2]
    return accumulated / weight_sum


def body(
    hidden,
    lengths,
    prefix_id,
    placement_perm,
    prefix_owner,
    prefix_cache,
    qkv_weight,
    q_gain,
    k_gain,
    out_weight,
    attn_gain,
    gate_up_weight,
    down_weight,
    mlp_gain,
):
    tensor_rank = lax.axis_index("tensor")
    group_index = lax.axis_index("dp")
    slot_ids, live_slots, owner_req, offsets, prefix_pick = slot_plan(
        lengths, prefix_id, placement_perm, group_index
    )
    local_rows = hidden.shape[0]
    local_width = qkv_weight.shape[2]
    local_heads = local_width // HD
    assert local_heads == 1
    row_start = tensor_rank * local_rows
    column_start = tensor_rank * local_width
    score_scale = HD ** (-0.5)
    both_prefixes, hidden = fetch_prefixes(prefix_cache[0], prefix_owner, hidden)
    full_rows = ag_tensor(hidden)
    projected = jnp.einsum("cd,kde->kce", full_rows, qkv_weight, preferred_element_type=jnp.float32)
    norm_gains = jnp.stack(
        [
            lax.dynamic_slice_in_dim(q_gain, column_start, local_width),
            lax.dynamic_slice_in_dim(k_gain, column_start, local_width),
        ]
    )
    squares = jnp.sum(projected[:2] * projected[:2], axis=2)
    totals = psum_tensor_f32(squares)
    normed = projected[:2] * lax.rsqrt(totals / D + EPSILON)[:, :, None] * norm_gains[:, None, :]
    queries = rotate(normed[0].reshape(CAP, local_heads, HD), offsets).astype(jnp.bfloat16)
    key_heads = rotate(normed[1].reshape(CAP, local_heads, HD), offsets).astype(jnp.bfloat16)
    value_heads = projected[2].astype(jnp.bfloat16).reshape(CAP, local_heads, HD)
    suf_scores = (
        jnp.einsum("chd,khd->hck", queries, key_heads, preferred_element_type=jnp.float32)
        * score_scale
    )
    visible = (
        (owner_req[:, None] == owner_req[None, :])
        & live_slots[None, :]
        & (slot_ids[None, :] <= slot_ids[:, None])
    )
    suf_scores = jnp.where(visible[None], suf_scores, MASKED_SCORE)
    partials = [partial_softmax(suf_scores, value_heads)]
    top, total, acc = prefix_attention(queries.reshape(CAP, HD), both_prefixes, prefix_pick)
    partials.append((top[None], total[None], acc[None]))
    attended = merge_partials(partials).astype(jnp.bfloat16)
    attended = attended.transpose(1, 0, 2).reshape(CAP, local_width)
    by_core = attended.reshape((4, 2, 2, -1) + attended.shape[1:])
    my_core = tensor_coords()[2]

    def project(rows):
        flat = jnp.dot(rows.reshape(-1, rows.shape[-1]), out_weight, preferred_element_type=jnp.float32)
        return flat.astype(jnp.bfloat16).reshape(rows.shape[:-1] + (out_weight.shape[1],))

    summed = rs_tensor_halves(
        project(jnp.take(by_core, my_core, axis=2)), project(jnp.take(by_core, 1 - my_core, axis=2))
    )
    mid_rows = (hidden.astype(jnp.float32) + rms_scale(summed, attn_gain)).astype(jnp.bfloat16)
    quad, mate = ag_tensor_halves(mid_rows)

    def mlp_part(rows):
        flat = rows.reshape(-1, rows.shape[-1])
        gate_up = jnp.einsum("cd,kdf->kcf", flat, gate_up_weight, preferred_element_type=jnp.float32)
        activated = (jax.nn.silu(gate_up[0]) * gate_up[1]).astype(jnp.bfloat16)
        down = jnp.dot(activated, down_weight, preferred_element_type=jnp.float32)
        return down.astype(jnp.bfloat16).reshape(rows.shape)

    mlp_term = rs_tensor_halves(mlp_part(quad), mlp_part(mate))
    result = mid_rows.astype(jnp.float32) + rms_scale(mlp_term, mlp_gain)
    live_rows = lax.dynamic_slice_in_dim(live_slots, row_start, local_rows, 0)
    hidden_out = jnp.where(live_rows[:, None], result, 0.0).astype(jnp.bfloat16)
    key_out = jnp.where(live_slots[:, None], key_heads.reshape(CAP, local_width), 0.0)
    value_out = jnp.where(live_slots[:, None], value_heads.reshape(CAP, local_width), 0.0)
    suffix_kv = jnp.stack([key_out, value_out])
    return (hidden_out, suffix_kv)


def solution(mesh):
    in_specs = (
        P(("dp", "tensor"), None),
        P(),
        P(),
        P(),
        P(),
        P("dp", None, None, "tensor"),
        P(None, None, "tensor"),
        P(),
        P(),
        P("tensor", None),
        P(),
        P(None, None, "tensor"),
        P("tensor", None),
        P(),
    )
    out_specs = (P(("dp", "tensor"), None), P(None, "dp", "tensor"))
    return jax.shard_map(body, mesh=mesh, in_specs=in_specs, out_specs=out_specs, check_vma=False)
```
